32 devices in a mesh: row: 8 (over z, x), col: 4 (over y, core).
Axes of the slice: x: 2, y: 2, z: 4, core: 2. Of those that a mesh axis runs over, the one named last changes fastest.
Arguments:
- probe: float32 [32768, 128], P(('row', 'col'))
- self_weight: float32 [32768], P('row'), may hold values from 1.5 to 3
- blocks: float32 [4096, 128, 128], P(('row', 'col')), may hold values from -0.078125 to 0.078125
- block_row: int32 [4096], P(('row', 'col')), may hold values from 0 to 31
- block_col: int32 [4096], P(('row', 'col')), may hold values from 0 to 63
- counts: int32 [32], P(('row', 'col')), may hold values from 1 to 128, as said below
Outputs:
- projected: float32 [32768, 128], P(('row', 'col'))
- basis: float32 [32768, 128], P(('row', 'col'))
The draws below stay inside these ranges and needn't reach their ends.
Inputs may be any that keep to these rules, and one draw needn't show every extreme that they name: Slots 0 to counts[g] - 1 of group g are live, the rest hold values that do not count; in every draw some group has all 128 slots live.
All inputs are finite; a program needn't handle non-finite values.
Results may differ from the reference program's by a relative error of at most 0.0001.
Values sent between devices are 32-bit elements; how exact they have to be, the bound alone decides.
No kernel may reach another device: no remote copies, remote signals or barrier semaphores. Data moves between devices by JAX's collectives and lax.ppermute only.
A program may use at most 128 MiB of HBM per device.

```python
import math
import jax
import jax.numpy as jnp
from jax import lax

BS = 128
P_SIZE = 128
NBR_DEV = 32
K = 128
CB_DEV = 8
STRIPE = 64
GROUPS = 32
NB = 256
N = 32768
KTOT = 4096
BPR = 8
N_COL = 4


def draw_probe(key, part):
    position = jnp.arange(N, dtype=jnp.float32) / N
    values = jax.random.normal(key, (N, P_SIZE), jnp.float32)
    scale = 10.0 ** position
    return values * scale[:, None]


def draw_counts(key, part):
    first, second = jax.random.split(key)
    divisor = jax.random.randint(first, (GROUPS,), 1, 7)
    filled = jnp.maximum(K // divisor, 1)
    where = jax.random.randint(second, (), 0, GROUPS)
    return filled.at[where].set(K).astype(jnp.int32)


def set_ends(values, key, low, high):
    longest = values.shape.index(max(values.shape))
    spots = []
    for shift in (0, 1):
        where = [jax.random.randint(jax.random.fold_in(key, axis), (), 0, length) for axis, length in enumerate(values.shape)]
        where[longest] = (where[longest] + shift) % values.shape[longest]
        spots.append(tuple(where))
    return values.at[spots[0]].set(low).at[spots[1]].set(high)


def block_scale(stream_key, extent, pieces, least, largest):
    gain, own = 1.0, jax.random.fold_in(stream_key, 6)
    for axis_at, blocks in pieces:
        draws = jnp.exp(jax.random.uniform(jax.random.fold_in(own, axis_at), (blocks,), jnp.float32, least / len(pieces), largest / len(pieces)))
        gain = gain * jnp.repeat(draws, extent[axis_at] // blocks).reshape([-1 if axis == axis_at else 1 for axis in range(len(extent))])
    return gain


def scatter_about(key, shape, scale, most, cuts=(), kind=jnp.bfloat16):
    loudness = block_scale(key, shape, cuts, -0.22, 0.18) if cuts else 1.0
    result = jax.random.normal(key, shape, jnp.float32) * scale * loudness
    return jnp.minimum(jnp.maximum(result, -most), most).astype(kind)


def setup_inputs(seed: int = 0) -> dict:
    key_of = jax.random.split(jax.random.key(seed), 7)
    return {
        "probe": draw_probe(jax.random.fold_in(key_of[6], 71), 0),
        "self_weight": jnp.clip(1.5 + 1.5 * jax.random.uniform(key_of[1], (N,), jnp.float32) ** block_scale(key_of[1], (N,), ((0, 8),), -0.2, 0.2), 1.5, 3.0),
        "blocks": scatter_about(key_of[2], (KTOT, BS, BS), (6 * BS * BPR) ** -0.5, 0.078125, ((0, 32),), jnp.float32),
        "block_row": set_ends(jax.random.randint(key_of[3], (KTOT,), 0, NBR_DEV), jax.random.fold_in(key_of[3], 1), 0, NBR_DEV - 1).astype(jnp.int32),
        "block_col": set_ends(jax.random.randint(key_of[4], (KTOT,), 0, STRIPE), jax.random.fold_in(key_of[4], 1), 0, STRIPE - 1).astype(jnp.int32),
        "counts": draw_counts(jax.random.fold_in(key_of[6], 71), 0),
    }


PRECISE = lax.Precision.HIGHEST

def reference(probe, self_weight, blocks, block_row, block_col, counts):
    probe_blocks = probe.reshape(NB, BS, P_SIZE)
    live_mask = (jnp.arange(K)[None, :] < counts[:, None]).astype(jnp.float32)
    groups = jnp.arange(GROUPS, dtype=jnp.int32)
    owners = groups // N_COL
    stripes = groups % N_COL
    global_row = owners[:, None] * NBR_DEV + block_row.reshape(GROUPS, K)
    local_col = block_col.reshape(GROUPS, K)
    slot_col = (local_col // CB_DEV * N_COL + stripes[:, None]) * CB_DEV + local_col % CB_DEV
    slot_col = slot_col.astype(jnp.int32)
    group_vals = blocks.reshape(GROUPS, K, BS, BS)

    def forward(totals, slot_item):
        block_vals, rows_here, cols_here, mask_here = slot_item
        products = jnp.einsum('kij,kjp->kip', block_vals, probe_blocks[cols_here], precision=PRECISE)
        return (totals.at[rows_here].add(products * mask_here[:, None, None]), None)
    sparse_part, _ = lax.scan(forward, jnp.zeros((NB, BS, P_SIZE), jnp.float32), (group_vals, global_row, slot_col, live_mask))
    projected = self_weight[:, None] * probe + sparse_part.reshape(N, P_SIZE)
    projected_blocks = projected.reshape(NB, BS, P_SIZE)

    def backward(totals, slot_item):
        block_vals, rows_here, cols_here, mask_here = slot_item
        products = jnp.einsum('kji,kjp->kip', block_vals, projected_blocks[rows_here], precision=PRECISE)
        return (totals.at[cols_here].add(products * mask_here[:, None, None]), None)
    sparse_back, _ = lax.scan(backward, jnp.zeros((NB, BS, P_SIZE), jnp.float32), (group_vals, global_row, slot_col, live_mask))
    sketch = self_weight[:, None] * projected + sparse_back.reshape(N, P_SIZE)
    gram = jnp.dot(sketch.T.astype(jnp.float32), sketch.astype(jnp.float32), precision=PRECISE, preferred_element_type=jnp.float32)
    lower = jnp.linalg.cholesky(gram)
    solved = lax.linalg.triangular_solve(lower, sketch, left_side=False, lower=True, transpose_a=True)
    basis = solved * math.sqrt(N)
    return (projected, basis)
```

```python
import math

import jax
import jax.numpy as jnp
from jax import lax
from jax.sharding import PartitionSpec as P

PRECISE = lax.Precision.HIGHEST


def shift_pairs(n, k):
    return [(i, (i + k) % n) for i in range(n)]


def ring_gather(x, axis, n):
    me = lax.axis_index(axis)
    parts = [x] + [lax.ppermute(x, axis, shift_pairs(n, -k)) for k in range(1, n)]
    return jnp.roll(jnp.stack(parts), me, axis=0).reshape(n * x.shape[0], *x.shape[1:])


def ring_reduce_scatter(x, axis, n):
    me = lax.axis_index(axis)
    chunks = x.reshape(n, x.shape[0] // n, *x.shape[1:])
    total = lax.dynamic_index_in_dim(chunks, me, 0, keepdims=False)
    for k in range(1, n):
        send = lax.dynamic_index_in_dim(chunks, (me + k) % n, 0, keepdims=False)
        total = total + lax.ppermute(send, axis, shift_pairs(n, k))
    return total


def butterfly_sum(x, axes, n):
    if n & (n - 1):
        return lax.psum(x, axes)
    step = 1
    while step < n:
        x = x + lax.ppermute(x, axes, [(i, i ^ step) for i in range(n)])
        step *= 2
    return x


def shards(probe, self_weight, blocks, block_row, block_col, counts):
    col_count = lax.axis_size("col")
    row_count = lax.axis_size("row")
    block_size = blocks.shape[1]
    probe_width = probe.shape[1]
    slot_count = blocks.shape[0]
    local_rows = probe.shape[0]
    owner_rows = local_rows * col_count
    owner_blocks = owner_rows // block_size
    stripe_rows = local_rows * row_count
    stripe_blocks = stripe_rows // block_size
    answers = local_rows * row_count * col_count
    stripe_probe = lax.all_gather(probe, "row", axis=0, tiled=True)
    probe_blocks = stripe_probe.reshape(stripe_blocks, block_size, probe_width)
    live_mask = (jnp.arange(slot_count) < counts[0]).astype(jnp.float32)
    row_select = (block_row[:, None] == jnp.arange(owner_blocks)[None, :]).astype(
        jnp.float32
    ) * live_mask[:, None]
    col_select = (block_col[:, None] == jnp.arange(stripe_blocks)[None, :]).astype(jnp.float32)
    picked = probe_blocks[block_col]
    products = jnp.einsum("kij,kjp->kip", blocks, picked, precision=PRECISE)
    partial_value = jnp.einsum("kr,kip->rip", row_select, products, precision=PRECISE).reshape(
        owner_rows, probe_width
    )
    local_start = lax.axis_index("col") * local_rows
    local_weight = lax.dynamic_slice_in_dim(self_weight, local_start, local_rows, 0)
    share_sum = ring_reduce_scatter(partial_value, "col", col_count)
    projected = local_weight[:, None] * probe + share_sum
    owner_y = ring_gather(projected, "col", col_count)
    y_blocks = owner_y.reshape(owner_blocks, block_size, probe_width)
    picked_y = jnp.einsum("kr,rip->kip", row_select, y_blocks, precision=PRECISE)
    transposed = jnp.einsum("kji,kjp->kip", blocks, picked_y, precision=PRECISE)
    w_partial = jnp.einsum("kc,kip->cip", col_select, transposed, precision=PRECISE).reshape(
        stripe_rows, probe_width
    )
    w_share = lax.psum_scatter(w_partial, "row", scatter_dimension=0, tiled=True)
    sketch = local_weight[:, None] * projected + w_share
    gram_part = jnp.dot(sketch.T, sketch, precision=PRECISE, preferred_element_type=jnp.float32)
    gram = butterfly_sum(gram_part, ("row", "col"), row_count * col_count)
    lower = jnp.linalg.cholesky(gram)
    solved = lax.linalg.triangular_solve(
        lower, sketch, left_side=False, lower=True, transpose_a=True
    )
    basis = solved * math.sqrt(answers)
    return (projected, basis)


def solution(mesh):
    in_specs = (
        P(("row", "col"), None),
        P("row"),
        P(("row", "col"), None, None),
        P(("row", "col")),
        P(("row", "col")),
        P(("row", "col")),
    )
    out_specs = (P(("row", "col"), None), P(("row", "col"), None))
    return jax.shard_map(shards, mesh=mesh, in_specs=in_specs, out_specs=out_specs, check_vma=False)
```

```python
import math

import jax
import jax.numpy as jnp
from jax import lax
from jax.sharding import PartitionSpec as P

PRECISE = lax.Precision.HIGHEST


def shift_pairs(n, k):
    return [(i, (i + k) % n) for i in range(n)]


def ring_gather(x, axis, n):
    me = lax.axis_index(axis)
    parts = [x] + [lax.ppermute(x, axis, shift_pairs(n, -k)) for k in range(1, n)]
    return jnp.roll(jnp.stack(parts), me, axis=0).reshape(n * x.shape[0], *x.shape[1:])


def ring_reduce_scatter(x, axis, n):
    me = lax.axis_index(axis)
    chunks = x.reshape(n, x.shape[0] // n, *x.shape[1:])
    total = lax.dynamic_index_in_dim(chunks, me, 0, keepdims=False)
    for k in range(1, n):
        send = lax.dynamic_index_in_dim(chunks, (me + k) % n, 0, keepdims=False)
        total = total + lax.ppermute(send, axis, shift_pairs(n, k))
    return total


def line_pairs(n, step, lo, hi):
    return [(i, i + step) for i in range(lo, hi) if 0 <= i + step < n]


def pair_line_gather(x, axis, n):
    if n % 2:
        return ring_gather(x, axis, n)
    me = lax.axis_index(axis)
    outer, inner = me // 2, me % 2
    groups = n // 2
    partner = lax.ppermute(x, axis, [(i, i ^ 1) for i in range(n)])
    pair = jnp.roll(jnp.stack([x, partner]), inner, axis=0)
    below, above = [], []
    for d in range(1, groups):
        above.append(lax.ppermute(pair, axis, line_pairs(n, -2 * d, 0, n)))
        below.append(lax.ppermute(pair, axis, line_pairs(n, 2 * d, 0, n)))
    line = jnp.stack(below[::-1] + [pair] + above)
    own = lax.dynamic_slice_in_dim(line, groups - 1 - outer, groups, 0)
    return own.reshape(n * x.shape[0], *x.shape[1:])


def pair_line_reduce_scatter(x, axis, n):
    if n % 2:
        return ring_reduce_scatter(x, axis, n)
    me = lax.axis_index(axis)
    outer, inner = me // 2, me % 2
    groups = n // 2
    rows = x.shape[0] // n
    chunks = x.reshape(groups, 2, rows, *x.shape[1:])
    total = lax.dynamic_index_in_dim(chunks, outer, 0, keepdims=False)
    for d in range(1, groups):
        up = lax.dynamic_index_in_dim(chunks, jnp.minimum(outer + d, groups - 1), 0, keepdims=False)
        down = lax.dynamic_index_in_dim(chunks, jnp.maximum(outer - d, 0), 0, keepdims=False)
        total = total + lax.ppermute(up, axis, line_pairs(n, 2 * d, 0, n))
        total = total + lax.ppermute(down, axis, line_pairs(n, -2 * d, 0, n))
    keep = lax.dynamic_index_in_dim(total, inner, 0, keepdims=False)
    give = lax.dynamic_index_in_dim(total, 1 - inner, 0, keepdims=False)
    return keep + lax.ppermute(give, axis, [(i, i ^ 1) for i in range(n)])


def butterfly_sum(x, axes, n):
    if n & (n - 1):
        return lax.psum(x, axes)
    step = 1
    while step < n:
        x = x + lax.ppermute(x, axes, [(i, i ^ step) for i in range(n)])
        step *= 2
    return x


def shards(probe, self_weight, blocks, block_row, block_col, counts):
    col_count = lax.axis_size("col")
    row_count = lax.axis_size("row")
    block_size = blocks.shape[1]
    probe_width = probe.shape[1]
    slot_count = blocks.shape[0]
    local_rows = probe.shape[0]
    owner_rows = local_rows * col_count
    owner_blocks = owner_rows // block_size
    stripe_rows = local_rows * row_count
    stripe_blocks = stripe_rows // block_size
    answers = local_rows * row_count * col_count
    stripe_probe = pair_line_gather(probe, "row", row_count)
    probe_blocks = stripe_probe.reshape(stripe_blocks, block_size, probe_width)
    live_mask = (jnp.arange(slot_count) < counts[0]).astype(jnp.float32)
    row_select = (block_row[:, None] == jnp.arange(owner_blocks)[None, :]).astype(
        jnp.float32
    ) * live_mask[:, None]
    col_select = (block_col[:, None] == jnp.arange(stripe_blocks)[None, :]).astype(jnp.float32)
    picked = probe_blocks[block_col]
    products = jnp.einsum("kij,kjp->kip", blocks, picked, precision=PRECISE)
    partial_value = jnp.einsum("kr,kip->rip", row_select, products, precision=PRECISE).reshape(
        owner_rows, probe_width
    )
    local_start = lax.axis_index("col") * local_rows
    local_weight = lax.dynamic_slice_in_dim(self_weight, local_start, local_rows, 0)
    share_sum = ring_reduce_scatter(partial_value, "col", col_count)
    projected = local_weight[:, None] * probe + share_sum
    owner_y = ring_gather(projected, "col", col_count)
    y_blocks = owner_y.reshape(owner_blocks, block_size, probe_width)
    picked_y = jnp.einsum("kr,rip->kip", row_select, y_blocks, precision=PRECISE)
    transposed = jnp.einsum("kji,kjp->kip", blocks, picked_y, precision=PRECISE)
    w_partial = jnp.einsum("kc,kip->cip", col_select, transposed, precision=PRECISE).reshape(
        stripe_rows, probe_width
    )
    w_share = pair_line_reduce_scatter(w_partial, "row", row_count)
    sketch = local_weight[:, None] * projected + w_share
    gram_part = jnp.dot(sketch.T, sketch, precision=PRECISE, preferred_element_type=jnp.float32)
    gram = butterfly_sum(gram_part, ("row", "col"), row_count * col_count)
    lower = jnp.linalg.cholesky(gram)
    solved = lax.linalg.triangular_solve(
        lower, sketch, left_side=False, lower=True, transpose_a=True
    )
    basis = solved * math.sqrt(answers)
    return (projected, basis)


def solution(mesh):
    in_specs = (
        P(("row", "col"), None),
        P("row"),
        P(("row", "col"), None, None),
        P(("row", "col")),
        P(("row", "col")),
        P(("row", "col")),
    )
    out_specs = (P(("row", "col"), None), P(("row", "col"), None))
    return jax.shard_map(shards, mesh=mesh, in_specs=in_specs, out_specs=out_specs, check_vma=False)
```

```python
import math

import jax
import jax.numpy as jnp
from jax import lax
from jax.sharding import PartitionSpec as P

PRECISE = lax.Precision.HIGHEST
CHUNKS = 2


def shift_pairs(n, k):
    return [(i, (i + k) % n) for i in range(n)]


def ring_gather(x, axis, n):
    me = lax.axis_index(axis)
    parts = [x] + [lax.ppermute(x, axis, shift_pairs(n, -k)) for k in range(1, n)]
    return jnp.roll(jnp.stack(parts), me, axis=0).reshape(n * x.shape[0], *x.shape[1:])


def ring_reduce_scatter(x, axis, n):
    me = lax.axis_index(axis)
    chunks = x.reshape(n, x.shape[0] // n, *x.shape[1:])
    total = lax.dynamic_index_in_dim(chunks, me, 0, keepdims=False)
    for k in range(1, n):
        send = lax.dynamic_index_in_dim(chunks, (me + k) % n, 0, keepdims=False)
        total = total + lax.ppermute(send, axis, shift_pairs(n, k))
    return total


def butterfly_sum(x, axes, n):
    if n & (n - 1):
        return lax.psum(x, axes)
    step = 1
    while step < n:
        x = x + lax.ppermute(x, axes, [(i, i ^ step) for i in range(n)])
        step *= 2
    return x


def shards(probe, self_weight, blocks, block_row, block_col, counts):
    col_count = lax.axis_size("col")
    row_count = lax.axis_size("row")
    block_size = blocks.shape[1]
    probe_width = probe.shape[1]
    slot_count = blocks.shape[0]
    local_rows = probe.shape[0]
    owner_rows = local_rows * col_count
    owner_blocks = owner_rows // block_size
    stripe_rows = local_rows * row_count
    stripe_blocks = stripe_rows // block_size
    answers = local_rows * row_count * col_count
    live_mask = (jnp.arange(slot_count) < counts[0]).astype(jnp.float32)
    row_select = (block_row[:, None] == jnp.arange(owner_blocks)[None, :]).astype(
        jnp.float32
    ) * live_mask[:, None]
    col_select = (block_col[:, None] == jnp.arange(stripe_blocks)[None, :]).astype(jnp.float32)
    local_start = lax.axis_index("col") * local_rows
    local_weight = lax.dynamic_slice_in_dim(self_weight, local_start, local_rows, 0)
    chunk_width = probe_width // CHUNKS if probe_width % CHUNKS == 0 else probe_width
    projected_parts, sketch_parts = [], []
    for first in range(0, probe_width, chunk_width):
        probe_part = probe[:, first : first + chunk_width]
        stripe_probe = lax.all_gather(probe_part, "row", axis=0, tiled=True)
        probe_blocks = stripe_probe.reshape(stripe_blocks, block_size, chunk_width)
        picked = probe_blocks[block_col]
        products = jnp.einsum("kij,kjp->kip", blocks, picked, precision=PRECISE)
        partial_value = jnp.einsum(
            "kr,kip->rip", row_select, products, precision=PRECISE
        ).reshape(owner_rows, chunk_width)
        share_sum = ring_reduce_scatter(partial_value, "col", col_count)
        projected_part = local_weight[:, None] * probe_part + share_sum
        owner_y = ring_gather(projected_part, "col", col_count)
        y_blocks = owner_y.reshape(owner_blocks, block_size, chunk_width)
        picked_y = jnp.einsum("kr,rip->kip", row_select, y_blocks, precision=PRECISE)
        transposed = jnp.einsum("kji,kjp->kip", blocks, picked_y, precision=PRECISE)
        w_partial = jnp.einsum(
            "kc,kip->cip", col_select, transposed, precision=PRECISE
        ).reshape(stripe_rows, chunk_width)
        w_share = lax.psum_scatter(w_partial, "row", scatter_dimension=0, tiled=True)
        projected_parts.append(projected_part)
        sketch_parts.append(local_weight[:, None] * projected_part + w_share)
    projected = jnp.concatenate(projected_parts, axis=1)
    sketch = jnp.concatenate(sketch_parts, axis=1)
    gram_part = jnp.dot(sketch.T, sketch, precision=PRECISE, preferred_element_type=jnp.float32)
    gram = butterfly_sum(gram_part, ("row", "col"), row_count * col_count)
    lower = jnp.linalg.cholesky(gram)
    solved = lax.linalg.triangular_solve(
        lower, sketch, left_side=False, lower=True, transpose_a=True
    )
    basis = solved * math.sqrt(answers)
    return (projected, basis)


def solution(mesh):
    in_specs = (
        P(("row", "col"), None),
        P("row"),
        P(("row", "col"), None, None),
        P(("row", "col")),
        P(("row", "col")),
        P(("row", "col")),
    )
    out_specs = (P(("row", "col"), None), P(("row", "col"), None))
    return jax.shard_map(shards, mesh=mesh, in_specs=in_specs, out_specs=out_specs, check_vma=False)
```

```python
import math

import jax
import jax.numpy as jnp
from jax import lax
from jax.sharding import PartitionSpec as P

PRECISE = lax.Precision.HIGHEST
BLOCK_PRECISION = lax.Precision.HIGH


def shift_pairs(n, k):
    return [(i, (i + k) % n) for i in range(n)]


def ring_gather(x, axis, n):
    me = lax.axis_index(axis)
    parts = [x] + [lax.ppermute(x, axis, shift_pairs(n, -k)) for k in range(1, n)]
    return jnp.roll(jnp.stack(parts), me, axis=0).reshape(n * x.shape[0], *x.shape[1:])


def ring_reduce_scatter(x, axis, n):
    me = lax.axis_index(axis)
    chunks = x.reshape(n, x.shape[0] // n, *x.shape[1:])
    total = lax.dynamic_index_in_dim(chunks, me, 0, keepdims=False)
    for k in range(1, n):
        send = lax.dynamic_index_in_dim(chunks, (me + k) % n, 0, keepdims=False)
        total = total + lax.ppermute(send, axis, shift_pairs(n, k))
    return total


def butterfly_sum(x, axes, n):
    if n & (n - 1):
        return lax.psum(x, axes)
    step = 1
    while step < n:
        x = x + lax.ppermute(x, axes, [(i, i ^ step) for i in range(n)])
        step *= 2
    return x


def shards(probe, self_weight, blocks, block_row, block_col, counts):
    col_count = lax.axis_size("col")
    row_count = lax.axis_size("row")
    block_size = blocks.shape[1]
    probe_width = probe.shape[1]
    slot_count = blocks.shape[0]
    local_rows = probe.shape[0]
    owner_rows = local_rows * col_count
    owner_blocks = owner_rows // block_size
    stripe_rows = local_rows * row_count
    stripe_blocks = stripe_rows // block_size
    answers = local_rows * row_count * col_count
    stripe_probe = lax.all_gather(probe, "row", axis=0, tiled=True)
    probe_blocks = stripe_probe.reshape(stripe_blocks, block_size, probe_width)
    live_mask = (jnp.arange(slot_count) < counts[0]).astype(jnp.float32)
    row_select = (block_row[:, None] == jnp.arange(owner_blocks)[None, :]).astype(
        jnp.float32
    ) * live_mask[:, None]
    col_select = (block_col[:, None] == jnp.arange(stripe_blocks)[None, :]).astype(jnp.float32)
    picked = probe_blocks[block_col]
    products = jnp.einsum("kij,kjp->kip", blocks, picked, precision=BLOCK_PRECISION)
    partial_value = lax.dot_general(
        row_select,
        products.reshape(slot_count, block_size * probe_width),
        (((0,), (0,)), ((), ())),
        precision=PRECISE,
    ).reshape(owner_rows, probe_width)
    local_start = lax.axis_index("col") * local_rows
    local_weight = lax.dynamic_slice_in_dim(self_weight, local_start, local_rows, 0)
    share_sum = ring_reduce_scatter(partial_value, "col", col_count)
    projected = local_weight[:, None] * probe + share_sum
    owner_y = ring_gather(projected, "col", col_count)
    y_blocks = owner_y.reshape(owner_blocks, block_size, probe_width)
    picked_y = jnp.dot(
        row_select, y_blocks.reshape(owner_blocks, block_size * probe_width), precision=PRECISE
    ).reshape(slot_count, block_size, probe_width)
    transposed = jnp.einsum("kji,kjp->kip", blocks, picked_y, precision=BLOCK_PRECISION)
    w_partial = lax.dot_general(
        col_select,
        transposed.reshape(slot_count, block_size * probe_width),
        (((0,), (0,)), ((), ())),
        precision=PRECISE,
    ).reshape(stripe_rows, probe_width)
    w_share = lax.psum_scatter(w_partial, "row", scatter_dimension=0, tiled=True)
    sketch = local_weight[:, None] * projected + w_share
    gram_part = jnp.dot(sketch.T, sketch, precision=PRECISE, preferred_element_type=jnp.float32)
    gram = butterfly_sum(gram_part, ("row", "col"), row_count * col_count)
    lower = jnp.linalg.cholesky(gram)
    solved = lax.linalg.triangular_solve(
        lower, sketch, left_side=False, lower=True, transpose_a=True
    )
    basis = solved * math.sqrt(answers)
    return (projected, basis)


def solution(mesh):
    in_specs = (
        P(("row", "col"), None),
        P("row"),
        P(("row", "col"), None, None),
        P(("row", "col")),
        P(("row", "col")),
        P(("row", "col")),
    )
    out_specs = (P(("row", "col"), None), P(("row", "col"), None))
    return jax.shard_map(shards, mesh=mesh, in_specs=in_specs, out_specs=out_specs, check_vma=False)
```

```python
import math

import jax
import jax.numpy as jnp
from jax import lax
from jax.experimental import pallas as pl
from jax.experimental.pallas import tpu as pltpu
from jax.sharding import PartitionSpec as P

PRECISE = lax.Precision.HIGHEST
INTERPRET = False


def shift_pairs(n, k):
    return [(i, (i + k) % n) for i in range(n)]


def ring_gather(x, axis, n):
    me = lax.axis_index(axis)
    parts = [x] + [lax.ppermute(x, axis, shift_pairs(n, -k)) for k in range(1, n)]
    return jnp.roll(jnp.stack(parts), me, axis=0).reshape(n * x.shape[0], *x.shape[1:])


def ring_reduce_scatter(x, axis, n):
    me = lax.axis_index(axis)
    chunks = x.reshape(n, x.shape[0] // n, *x.shape[1:])
    total = lax.dynamic_index_in_dim(chunks, me, 0, keepdims=False)
    for k in range(1, n):
        send = lax.dynamic_index_in_dim(chunks, (me + k) % n, 0, keepdims=False)
        total = total + lax.ppermute(send, axis, shift_pairs(n, k))
    return total


def butterfly_sum(x, axes, n):
    if n & (n - 1):
        return lax.psum(x, axes)
    step = 1
    while step < n:
        x = x + lax.ppermute(x, axes, [(i, i ^ step) for i in range(n)])
        step *= 2
    return x


def slot_product(blocks, source, block_row, block_col, counts, out_rows, transpose):
    slot_count, block_size = blocks.shape[0], blocks.shape[1]
    width = source.shape[1]
    group = 8 if slot_count % 8 == 0 else 1

    def kernel(row_ref, col_ref, count_ref, block_ref, source_ref, out_ref):
        step = pl.program_id(0)

        @pl.when(step == 0)
        def _():
            out_ref[...] = jnp.zeros_like(out_ref)

        def body(s, carry):
            slot = step * group + s
            read = row_ref[slot] if transpose else col_ref[slot]
            write = col_ref[slot] if transpose else row_ref[slot]

            @pl.when(slot < count_ref[0])
            def _():
                piece = source_ref[pl.ds(pl.multiple_of(read * block_size, block_size), block_size), :]
                block = block_ref[s]
                if transpose:
                    block = block.T
                product = jnp.dot(
                    block, piece, precision=PRECISE, preferred_element_type=jnp.float32
                )
                at = pl.ds(pl.multiple_of(write * block_size, block_size), block_size)
                out_ref[at, :] = out_ref[at, :] + product

            return carry

        lax.fori_loop(0, group, body, 0, unroll=True)

    grid_spec = pltpu.PrefetchScalarGridSpec(
        num_scalar_prefetch=3,
        grid=(slot_count // group,),
        in_specs=[
            pl.BlockSpec((group, block_size, block_size), lambda g, *_: (g, 0, 0)),
            pl.BlockSpec(source.shape, lambda g, *_: (0, 0)),
        ],
        out_specs=pl.BlockSpec((out_rows, width), lambda g, *_: (0, 0)),
    )
    return pl.pallas_call(
        kernel,
        grid_spec=grid_spec,
        out_shape=jax.ShapeDtypeStruct((out_rows, width), jnp.float32),
        compiler_params=pltpu.CompilerParams(
            dimension_semantics=("arbitrary",), vmem_limit_bytes=48 * 1024 * 1024
        ),
        interpret=INTERPRET,
    )(block_row, block_col, counts, blocks, source)


def shards(probe, self_weight, blocks, block_row, block_col, counts):
    col_count = lax.axis_size("col")
    row_count = lax.axis_size("row")
    block_size = blocks.shape[1]
    probe_width = probe.shape[1]
    slot_count = blocks.shape[0]
    local_rows = probe.shape[0]
    owner_rows = local_rows * col_count
    owner_blocks = owner_rows // block_size
    stripe_rows = local_rows * row_count
    stripe_blocks = stripe_rows // block_size
    answers = local_rows * row_count * col_count
    stripe_probe = lax.all_gather(probe, "row", axis=0, tiled=True)
    partial_value = slot_product(
        blocks, stripe_probe, block_row, block_col, counts, owner_rows, False
    )
    local_start = lax.axis_index("col") * local_rows
    local_weight = lax.dynamic_slice_in_dim(self_weight, local_start, local_rows, 0)
    share_sum = ring_reduce_scatter(partial_value, "col", col_count)
    projected = local_weight[:, None] * probe + share_sum
    owner_y = ring_gather(projected, "col", col_count)
    w_partial = slot_product(blocks, owner_y, block_row, block_col, counts, stripe_rows, True)
    w_share = lax.psum_scatter(w_partial, "row", scatter_dimension=0, tiled=True)
    sketch = local_weight[:, None] * projected + w_share
    gram_part = jnp.dot(sketch.T, sketch, precision=PRECISE, preferred_element_type=jnp.float32)
    gram = butterfly_sum(gram_part, ("row", "col"), row_count * col_count)
    lower = jnp.linalg.cholesky(gram)
    solved = lax.linalg.triangular_solve(
        lower, sketch, left_side=False, lower=True, transpose_a=True
    )
    basis = solved * math.sqrt(answers)
    return (projected, basis)


def solution(mesh):
    in_specs = (
        P(("row", "col"), None),
        P("row"),
        P(("row", "col"), None, None),
        P(("row", "col")),
        P(("row", "col")),
        P(("row", "col")),
    )
    out_specs = (P(("row", "col"), None), P(("row", "col"), None))
    return jax.shard_map(shards, mesh=mesh, in_specs=in_specs, out_specs=out_specs, check_vma=False)
```

```python
import math

import jax
import jax.numpy as jnp
from jax import lax
from jax.experimental import pallas as pl
from jax.experimental.pallas import tpu as pltpu
from jax.sharding import PartitionSpec as P

PRECISE = lax.Precision.HIGHEST
INTERPRET = False


def shift_pairs(n, k):
    return [(i, (i + k) % n) for i in range(n)]


def ring_gather(x, axis, n):
    me = lax.axis_index(axis)
    parts = [x] + [lax.ppermute(x, axis, shift_pairs(n, -k)) for k in range(1, n)]
    return jnp.roll(jnp.stack(parts), me, axis=0).reshape(n * x.shape[0], *x.shape[1:])


def ring_reduce_scatter(x, axis, n):
    me = lax.axis_index(axis)
    chunks = x.reshape(n, x.shape[0] // n, *x.shape[1:])
    total = lax.dynamic_index_in_dim(chunks, me, 0, keepdims=False)
    for k in range(1, n):
        send = lax.dynamic_index_in_dim(chunks, (me + k) % n, 0, keepdims=False)
        total = total + lax.ppermute(send, axis, shift_pairs(n, k))
    return total


def group_sum(x, axis, n):
    me = lax.axis_index(axis)
    parts = [x] + [lax.ppermute(x, axis, shift_pairs(n, -k)) for k in range(1, n)]
    return jnp.sum(jnp.roll(jnp.stack(parts), me, axis=0), axis=0)


def butterfly_sum(x, axes, n):
    if n & (n - 1):
        return lax.psum(x, axes)
    step = 1
    while step < n:
        x = x + lax.ppermute(x, axes, [(i, i ^ step) for i in range(n)])
        step *= 2
    return x


def slot_product(blocks, source, block_row, block_col, counts, out_rows, transpose):
    slot_count, block_size = blocks.shape[0], blocks.shape[1]
    width = source.shape[1]
    group = 8 if slot_count % 8 == 0 else 1

    def kernel(row_ref, col_ref, count_ref, block_ref, source_ref, out_ref):
        step = pl.program_id(0)

        @pl.when(step == 0)
        def _():
            out_ref[...] = jnp.zeros_like(out_ref)

        def body(s, carry):
            slot = step * group + s
            read = row_ref[slot] if transpose else col_ref[slot]
            write = col_ref[slot] if transpose else row_ref[slot]

            @pl.when(slot < count_ref[0])
            def _():
                piece = source_ref[pl.ds(pl.multiple_of(read * block_size, block_size), block_size), :]
                block = block_ref[s]
                if transpose:
                    block = block.T
                product = jnp.dot(
                    block, piece, precision=PRECISE, preferred_element_type=jnp.float32
                )
                at = pl.ds(pl.multiple_of(write * block_size, block_size), block_size)
                out_ref[at, :] = out_ref[at, :] + product

            return carry

        lax.fori_loop(0, group, body, 0, unroll=True)

    grid_spec = pltpu.PrefetchScalarGridSpec(
        num_scalar_prefetch=3,
        grid=(slot_count // group,),
        in_specs=[
            pl.BlockSpec((group, block_size, block_size), lambda g, *_: (g, 0, 0)),
            pl.BlockSpec(source.shape, lambda g, *_: (0, 0)),
        ],
        out_specs=pl.BlockSpec((out_rows, width), lambda g, *_: (0, 0)),
    )
    return pl.pallas_call(
        kernel,
        grid_spec=grid_spec,
        out_shape=jax.ShapeDtypeStruct((out_rows, width), jnp.float32),
        compiler_params=pltpu.CompilerParams(
            dimension_semantics=("arbitrary",), vmem_limit_bytes=48 * 1024 * 1024
        ),
        interpret=INTERPRET,
    )(block_row, block_col, counts, blocks, source)


def shards(probe, self_weight, blocks, block_row, block_col, counts):
    col_count = lax.axis_size("col")
    row_count = lax.axis_size("row")
    block_size = blocks.shape[1]
    probe_width = probe.shape[1]
    slot_count = blocks.shape[0]
    local_rows = probe.shape[0]
    owner_rows = local_rows * col_count
    owner_blocks = owner_rows // block_size
    stripe_rows = local_rows * row_count
    stripe_blocks = stripe_rows // block_size
    answers = local_rows * row_count * col_count
    stripe_probe = lax.all_gather(probe, "row", axis=0, tiled=True)
    partial_value = slot_product(
        blocks, stripe_probe, block_row, block_col, counts, owner_rows, False
    )
    local_start = lax.axis_index("col") * local_rows
    local_weight = lax.dynamic_slice_in_dim(self_weight, local_start, local_rows, 0)
    share_sum = ring_reduce_scatter(partial_value, "col", col_count)
    projected = local_weight[:, None] * probe + share_sum
    owner_y = ring_gather(projected, "col", col_count)
    w_partial = slot_product(blocks, owner_y, block_row, block_col, counts, stripe_rows, True)
    w_share = lax.psum_scatter(w_partial, "row", scatter_dimension=0, tiled=True)
    sketch = local_weight[:, None] * projected + w_share
    gram_part = jnp.dot(sketch.T, sketch, precision=PRECISE, preferred_element_type=jnp.float32)
    gram = group_sum(group_sum(gram_part, "col", col_count), "row", row_count)
    lower = jnp.linalg.cholesky(gram)
    solved = lax.linalg.triangular_solve(
        lower, sketch, left_side=False, lower=True, transpose_a=True
    )
    basis = solved * math.sqrt(answers)
    return (projected, basis)


def solution(mesh):
    in_specs = (
        P(("row", "col"), None),
        P("row"),
        P(("row", "col"), None, None),
        P(("row", "col")),
        P(("row", "col")),
        P(("row", "col")),
    )
    out_specs = (P(("row", "col"), None), P(("row", "col"), None))
    return jax.shard_map(shards, mesh=mesh, in_specs=in_specs, out_specs=out_specs, check_vma=False)
```

```python
import math

import jax
import jax.numpy as jnp
from jax import lax
from jax.experimental import pallas as pl
from jax.experimental.pallas import tpu as pltpu
from jax.sharding import PartitionSpec as P

PRECISE = lax.Precision.HIGHEST
INTERPRET = False


def shift_pairs(n, k):
    return [(i, (i + k) % n) for i in range(n)]


def ring_gather(x, axis, n):
    me = lax.axis_index(axis)
    parts = [x] + [lax.ppermute(x, axis, shift_pairs(n, -k)) for k in range(1, n)]
    return jnp.roll(jnp.stack(parts), me, axis=0).reshape(n * x.shape[0], *x.shape[1:])


def ring_reduce_scatter(x, axis, n):
    me = lax.axis_index(axis)
    chunks = x.reshape(n, x.shape[0] // n, *x.shape[1:])
    total = lax.dynamic_index_in_dim(chunks, me, 0, keepdims=False)
    for k in range(1, n):
        send = lax.dynamic_index_in_dim(chunks, (me + k) % n, 0, keepdims=False)
        total = total + lax.ppermute(send, axis, shift_pairs(n, k))
    return total


def pair_all_reduce(x, axis, n):
    groups = n // 2
    if n % 2 or groups & (groups - 1):
        return lax.psum(x, axis)
    inner = lax.axis_index(axis) % 2
    halves = x.reshape(2, x.shape[0] // 2, *x.shape[1:])
    keep = lax.dynamic_index_in_dim(halves, inner, 0, keepdims=False)
    give = lax.dynamic_index_in_dim(halves, 1 - inner, 0, keepdims=False)
    part = keep + lax.ppermute(give, axis, [(i, i ^ 1) for i in range(n)])
    step = 2
    while step < n:
        part = part + lax.ppermute(part, axis, [(i, i ^ step) for i in range(n)])
        step *= 2
    other = lax.ppermute(part, axis, [(i, i ^ 1) for i in range(n)])
    return jnp.roll(jnp.stack([part, other]), inner, axis=0).reshape(x.shape)


def butterfly_sum(x, axes, n):
    if n & (n - 1):
        return lax.psum(x, axes)
    step = 1
    while step < n:
        x = x + lax.ppermute(x, axes, [(i, i ^ step) for i in range(n)])
        step *= 2
    return x


def slot_product(blocks, source, block_row, block_col, counts, out_rows, transpose):
    slot_count, block_size = blocks.shape[0], blocks.shape[1]
    width = source.shape[1]
    group = 8 if slot_count % 8 == 0 else 1

    def kernel(row_ref, col_ref, count_ref, block_ref, source_ref, out_ref):
        step = pl.program_id(0)

        @pl.when(step == 0)
        def _():
            out_ref[...] = jnp.zeros_like(out_ref)

        def body(s, carry):
            slot = step * group + s
            read = row_ref[slot] if transpose else col_ref[slot]
            write = col_ref[slot] if transpose else row_ref[slot]

            @pl.when(slot < count_ref[0])
            def _():
                piece = source_ref[pl.ds(pl.multiple_of(read * block_size, block_size), block_size), :]
                block = block_ref[s]
                if transpose:
                    block = block.T
                product = jnp.dot(
                    block, piece, precision=PRECISE, preferred_element_type=jnp.float32
                )
                at = pl.ds(pl.multiple_of(write * block_size, block_size), block_size)
                out_ref[at, :] = out_ref[at, :] + product

            return carry

        lax.fori_loop(0, group, body, 0, unroll=True)

    grid_spec = pltpu.PrefetchScalarGridSpec(
        num_scalar_prefetch=3,
        grid=(slot_count // group,),
        in_specs=[
            pl.BlockSpec((group, block_size, block_size), lambda g, *_: (g, 0, 0)),
            pl.BlockSpec(source.shape, lambda g, *_: (0, 0)),
        ],
        out_specs=pl.BlockSpec((out_rows, width), lambda g, *_: (0, 0)),
    )
    return pl.pallas_call(
        kernel,
        grid_spec=grid_spec,
        out_shape=jax.ShapeDtypeStruct((out_rows, width), jnp.float32),
        compiler_params=pltpu.CompilerParams(
            dimension_semantics=("arbitrary",), vmem_limit_bytes=48 * 1024 * 1024
        ),
        interpret=INTERPRET,
    )(block_row, block_col, counts, blocks, source)


def shards(probe, self_weight, blocks, block_row, block_col, counts):
    col_count = lax.axis_size("col")
    row_count = lax.axis_size("row")
    block_size = blocks.shape[1]
    probe_width = probe.shape[1]
    slot_count = blocks.shape[0]
    local_rows = probe.shape[0]
    owner_rows = local_rows * col_count
    owner_blocks = owner_rows // block_size
    stripe_rows = local_rows * row_count
    stripe_blocks = stripe_rows // block_size
    answers = local_rows * row_count * col_count
    stripe_probe = lax.all_gather(probe, "row", axis=0, tiled=True)
    partial_value = slot_product(
        blocks, stripe_probe, block_row, block_col, counts, owner_rows, False
    )
    local_start = lax.axis_index("col") * local_rows
    local_weight = lax.dynamic_slice_in_dim(self_weight, local_start, local_rows, 0)
    own_rows = lax.dynamic_slice_in_dim(partial_value, local_start, local_rows, 0)
    partial_value = lax.dynamic_update_slice_in_dim(
        partial_value, own_rows + local_weight[:, None] * probe, local_start, 0
    )
    owner_y = pair_all_reduce(partial_value, "col", col_count)
    projected = lax.dynamic_slice_in_dim(owner_y, local_start, local_rows, 0)
    w_partial = slot_product(blocks, owner_y, block_row, block_col, counts, stripe_rows, True)
    w_share = lax.psum_scatter(w_partial, "row", scatter_dimension=0, tiled=True)
    sketch = local_weight[:, None] * projected + w_share
    gram_part = jnp.dot(sketch.T, sketch, precision=PRECISE, preferred_element_type=jnp.float32)
    gram = butterfly_sum(gram_part, ("row", "col"), row_count * col_count)
    lower = jnp.linalg.cholesky(gram)
    solved = lax.linalg.triangular_solve(
        lower, sketch, left_side=False, lower=True, transpose_a=True
    )
    basis = solved * math.sqrt(answers)
    return (projected, basis)


def solution(mesh):
    in_specs = (
        P(("row", "col"), None),
        P("row"),
        P(("row", "col"), None, None),
        P(("row", "col")),
        P(("row", "col")),
        P(("row", "col")),
    )
    out_specs = (P(("row", "col"), None), P(("row", "col"), None))
    return jax.shard_map(shards, mesh=mesh, in_specs=in_specs, out_specs=out_specs, check_vma=False)
```

```python
import math

import jax
import jax.numpy as jnp
from jax import lax
from jax.experimental import pallas as pl
from jax.experimental.pallas import tpu as pltpu
from jax.sharding import PartitionSpec as P

PRECISE = lax.Precision.HIGHEST
INTERPRET = False
KERNEL_PRECISION = lax.Precision.HIGH


def shift_pairs(n, k):
    return [(i, (i + k) % n) for i in range(n)]


def ring_gather(x, axis, n):
    me = lax.axis_index(axis)
    parts = [x] + [lax.ppermute(x, axis, shift_pairs(n, -k)) for k in range(1, n)]
    return jnp.roll(jnp.stack(parts), me, axis=0).reshape(n * x.shape[0], *x.shape[1:])


def ring_reduce_scatter(x, axis, n):
    me = lax.axis_index(axis)
    chunks = x.reshape(n, x.shape[0] // n, *x.shape[1:])
    total = lax.dynamic_index_in_dim(chunks, me, 0, keepdims=False)
    for k in range(1, n):
        send = lax.dynamic_index_in_dim(chunks, (me + k) % n, 0, keepdims=False)
        total = total + lax.ppermute(send, axis, shift_pairs(n, k))
    return total


def pair_all_reduce(x, axis, n):
    groups = n // 2
    if n % 2 or groups & (groups - 1):
        return lax.psum(x, axis)
    inner = lax.axis_index(axis) % 2
    halves = x.reshape(2, x.shape[0] // 2, *x.shape[1:])
    keep = lax.dynamic_index_in_dim(halves, inner, 0, keepdims=False)
    give = lax.dynamic_index_in_dim(halves, 1 - inner, 0, keepdims=False)
    part = keep + lax.ppermute(give, axis, [(i, i ^ 1) for i in range(n)])
    step = 2
    while step < n:
        part = part + lax.ppermute(part, axis, [(i, i ^ step) for i in range(n)])
        step *= 2
    other = lax.ppermute(part, axis, [(i, i ^ 1) for i in range(n)])
    return jnp.roll(jnp.stack([part, other]), inner, axis=0).reshape(x.shape)


def butterfly_sum(x, axes, n):
    if n & (n - 1):
        return lax.psum(x, axes)
    step = 1
    while step < n:
        x = x + lax.ppermute(x, axes, [(i, i ^ step) for i in range(n)])
        step *= 2
    return x


def slot_product(blocks, source, block_row, block_col, counts, out_rows, transpose):
    slot_count, block_size = blocks.shape[0], blocks.shape[1]
    width = source.shape[1]
    group = 32 if slot_count % 32 == 0 else 1

    def kernel(row_ref, col_ref, count_ref, block_ref, source_ref, out_ref):
        step = pl.program_id(0)

        @pl.when(step == 0)
        def _():
            out_ref[...] = jnp.zeros_like(out_ref)

        def body(s, carry):
            slot = step * group + s
            read = row_ref[slot] if transpose else col_ref[slot]
            write = col_ref[slot] if transpose else row_ref[slot]

            @pl.when(slot < count_ref[0])
            def _():
                piece = source_ref[pl.ds(pl.multiple_of(read * block_size, block_size), block_size), :]
                block = block_ref[s]
                if transpose:
                    block = block.T
                product = jnp.dot(
                    block, piece, precision=KERNEL_PRECISION, preferred_element_type=jnp.float32
                )
                at = pl.ds(pl.multiple_of(write * block_size, block_size), block_size)
                out_ref[at, :] = out_ref[at, :] + product

            return carry

        lax.fori_loop(0, group, body, 0, unroll=True)

    grid_spec = pltpu.PrefetchScalarGridSpec(
        num_scalar_prefetch=3,
        grid=(slot_count // group,),
        in_specs=[
            pl.BlockSpec((group, block_size, block_size), lambda g, *_: (g, 0, 0)),
            pl.BlockSpec(source.shape, lambda g, *_: (0, 0)),
        ],
        out_specs=pl.BlockSpec((out_rows, width), lambda g, *_: (0, 0)),
    )
    return pl.pallas_call(
        kernel,
        grid_spec=grid_spec,
        out_shape=jax.ShapeDtypeStruct((out_rows, width), jnp.float32),
        compiler_params=pltpu.CompilerParams(
            dimension_semantics=("arbitrary",), vmem_limit_bytes=48 * 1024 * 1024
        ),
        interpret=INTERPRET,
    )(block_row, block_col, counts, blocks, source)


def shards(probe, self_weight, blocks, block_row, block_col, counts):
    col_count = lax.axis_size("col")
    row_count = lax.axis_size("row")
    block_size = blocks.shape[1]
    probe_width = probe.shape[1]
    slot_count = blocks.shape[0]
    local_rows = probe.shape[0]
    owner_rows = local_rows * col_count
    owner_blocks = owner_rows // block_size
    stripe_rows = local_rows * row_count
    stripe_blocks = stripe_rows // block_size
    answers = local_rows * row_count * col_count
    stripe_probe = lax.all_gather(probe, "row", axis=0, tiled=True)
    partial_value = slot_product(
        blocks, stripe_probe, block_row, block_col, counts, owner_rows, False
    )
    local_start = lax.axis_index("col") * local_rows
    local_weight = lax.dynamic_slice_in_dim(self_weight, local_start, local_rows, 0)
    own_rows = lax.dynamic_slice_in_dim(partial_value, local_start, local_rows, 0)
    partial_value = lax.dynamic_update_slice_in_dim(
        partial_value, own_rows + local_weight[:, None] * probe, local_start, 0
    )
    owner_y = pair_all_reduce(partial_value, "col", col_count)
    projected = lax.dynamic_slice_in_dim(owner_y, local_start, local_rows, 0)
    w_partial = slot_product(blocks, owner_y, block_row, block_col, counts, stripe_rows, True)
    w_share = lax.psum_scatter(w_partial, "row", scatter_dimension=0, tiled=True)
    sketch = local_weight[:, None] * projected + w_share
    gram_part = jnp.dot(sketch.T, sketch, precision=PRECISE, preferred_element_type=jnp.float32)
    gram = butterfly_sum(gram_part, ("row", "col"), row_count * col_count)
    lower = jnp.linalg.cholesky(gram)
    solved = lax.linalg.triangular_solve(
        lower, sketch, left_side=False, lower=True, transpose_a=True
    )
    basis = solved * math.sqrt(answers)
    return (projected, basis)


def solution(mesh):
    in_specs = (
        P(("row", "col"), None),
        P("row"),
        P(("row", "col"), None, None),
        P(("row", "col")),
        P(("row", "col")),
        P(("row", "col")),
    )
    out_specs = (P(("row", "col"), None), P(("row", "col"), None))
    return jax.shard_map(shards, mesh=mesh, in_specs=in_specs, out_specs=out_specs, check_vma=False)
```

```python
import math

import jax
import jax.numpy as jnp
from jax import lax
from jax.experimental import pallas as pl
from jax.experimental.pallas import tpu as pltpu
from jax.sharding import PartitionSpec as P

PRECISE = lax.Precision.HIGHEST
INTERPRET = False
KERNEL_PRECISION = lax.Precision.HIGH


def shift_pairs(n, k):
    return [(i, (i + k) % n) for i in range(n)]


def ring_gather(x, axis, n):
    me = lax.axis_index(axis)
    parts = [x] + [lax.ppermute(x, axis, shift_pairs(n, -k)) for k in range(1, n)]
    return jnp.roll(jnp.stack(parts), me, axis=0).reshape(n * x.shape[0], *x.shape[1:])


def ring_reduce_scatter(x, axis, n):
    me = lax.axis_index(axis)
    chunks = x.reshape(n, x.shape[0] // n, *x.shape[1:])
    total = lax.dynamic_index_in_dim(chunks, me, 0, keepdims=False)
    for k in range(1, n):
        send = lax.dynamic_index_in_dim(chunks, (me + k) % n, 0, keepdims=False)
        total = total + lax.ppermute(send, axis, shift_pairs(n, k))
    return total


def pair_all_reduce(x, axis, n):
    groups = n // 2
    if n % 2 or groups & (groups - 1):
        return lax.psum(x, axis)
    inner = lax.axis_index(axis) % 2
    halves = x.reshape(2, x.shape[0] // 2, *x.shape[1:])
    keep = lax.dynamic_index_in_dim(halves, inner, 0, keepdims=False)
    give = lax.dynamic_index_in_dim(halves, 1 - inner, 0, keepdims=False)
    part = keep + lax.ppermute(give, axis, [(i, i ^ 1) for i in range(n)])
    step = 2
    while step < n:
        part = part + lax.ppermute(part, axis, [(i, i ^ step) for i in range(n)])
        step *= 2
    other = lax.ppermute(part, axis, [(i, i ^ 1) for i in range(n)])
    return jnp.roll(jnp.stack([part, other]), inner, axis=0).reshape(x.shape)


def butterfly_sum(x, axes, n):
    if n & (n - 1):
        return lax.psum(x, axes)
    step = 1
    while step < n:
        x = x + lax.ppermute(x, axes, [(i, i ^ step) for i in range(n)])
        step *= 2
    return x


def slot_product(blocks, source, block_row, block_col, counts, out_rows, transpose):
    slot_count, block_size = blocks.shape[0], blocks.shape[1]
    width = source.shape[1]
    group = 32 if slot_count % 32 == 0 else 1

    def kernel(row_ref, col_ref, count_ref, block_ref, source_ref, out_ref):
        step = pl.program_id(0)

        @pl.when(step == 0)
        def _():
            out_ref[...] = jnp.zeros_like(out_ref)

        def body(s, carry):
            slot = step * group + s
            read = row_ref[slot] if transpose else col_ref[slot]
            write = col_ref[slot] if transpose else row_ref[slot]
            read = jnp.clip(read, 0, source_ref.shape[0] // block_size - 1)
            write = jnp.clip(write, 0, out_ref.shape[0] // block_size - 1)
            live = (slot < count_ref[0]).astype(jnp.float32)
            piece = source_ref[pl.ds(pl.multiple_of(read * block_size, block_size), block_size), :]
            block = block_ref[s]
            if transpose:
                block = block.T
            product = jnp.dot(
                block, piece, precision=KERNEL_PRECISION, preferred_element_type=jnp.float32
            )
            at = pl.ds(pl.multiple_of(write * block_size, block_size), block_size)
            out_ref[at, :] = out_ref[at, :] + product * live
            return carry

        lax.fori_loop(0, group, body, 0, unroll=True)

    grid_spec = pltpu.PrefetchScalarGridSpec(
        num_scalar_prefetch=3,
        grid=(slot_count // group,),
        in_specs=[
            pl.BlockSpec((group, block_size, block_size), lambda g, *_: (g, 0, 0)),
            pl.BlockSpec(source.shape, lambda g, *_: (0, 0)),
        ],
        out_specs=pl.BlockSpec((out_rows, width), lambda g, *_: (0, 0)),
    )
    return pl.pallas_call(
        kernel,
        grid_spec=grid_spec,
        out_shape=jax.ShapeDtypeStruct((out_rows, width), jnp.float32),
        compiler_params=pltpu.CompilerParams(
            dimension_semantics=("arbitrary",), vmem_limit_bytes=48 * 1024 * 1024
        ),
        interpret=INTERPRET,
    )(block_row, block_col, counts, blocks, source)


def shards(probe, self_weight, blocks, block_row, block_col, counts):
    col_count = lax.axis_size("col")
    row_count = lax.axis_size("row")
    block_size = blocks.shape[1]
    probe_width = probe.shape[1]
    slot_count = blocks.shape[0]
    local_rows = probe.shape[0]
    owner_rows = local_rows * col_count
    owner_blocks = owner_rows // block_size
    stripe_rows = local_rows * row_count
    stripe_blocks = stripe_rows // block_size
    answers = local_rows * row_count * col_count
    stripe_probe = lax.all_gather(probe, "row", axis=0, tiled=True)
    partial_value = slot_product(
        blocks, stripe_probe, block_row, block_col, counts, owner_rows, False
    )
    local_start = lax.axis_index("col") * local_rows
    local_weight = lax.dynamic_slice_in_dim(self_weight, local_start, local_rows, 0)
    own_rows = lax.dynamic_slice_in_dim(partial_value, local_start, local_rows, 0)
    partial_value = lax.dynamic_update_slice_in_dim(
        partial_value, own_rows + local_weight[:, None] * probe, local_start, 0
    )
    owner_y = pair_all_reduce(partial_value, "col", col_count)
    projected = lax.dynamic_slice_in_dim(owner_y, local_start, local_rows, 0)
    w_partial = slot_product(blocks, owner_y, block_row, block_col, counts, stripe_rows, True)
    w_share = lax.psum_scatter(w_partial, "row", scatter_dimension=0, tiled=True)
    sketch = local_weight[:, None] * projected + w_share
    gram_part = jnp.dot(sketch.T, sketch, precision=PRECISE, preferred_element_type=jnp.float32)
    gram = butterfly_sum(gram_part, ("row", "col"), row_count * col_count)
    lower = jnp.linalg.cholesky(gram)
    solved = lax.linalg.triangular_solve(
        lower, sketch, left_side=False, lower=True, transpose_a=True
    )
    basis = solved * math.sqrt(answers)
    return (projected, basis)


def solution(mesh):
    in_specs = (
        P(("row", "col"), None),
        P("row"),
        P(("row", "col"), None, None),
        P(("row", "col")),
        P(("row", "col")),
        P(("row", "col")),
    )
    out_specs = (P(("row", "col"), None), P(("row", "col"), None))
    return jax.shard_map(shards, mesh=mesh, in_specs=in_specs, out_specs=out_specs, check_vma=False)
```

```python
import math

import jax
import jax.numpy as jnp
from jax import lax
from jax.experimental import pallas as pl
from jax.experimental.pallas import tpu as pltpu
from jax.sharding import PartitionSpec as P

PRECISE = lax.Precision.HIGHEST
INTERPRET = False
KERNEL_PRECISION = lax.Precision.HIGH


def shift_pairs(n, k):
    return [(i, (i + k) % n) for i in range(n)]


def ring_gather(x, axis, n):
    me = lax.axis_index(axis)
    parts = [x] + [lax.ppermute(x, axis, shift_pairs(n, -k)) for k in range(1, n)]
    return jnp.roll(jnp.stack(parts), me, axis=0).reshape(n * x.shape[0], *x.shape[1:])


def ring_reduce_scatter(x, axis, n):
    me = lax.axis_index(axis)
    chunks = x.reshape(n, x.shape[0] // n, *x.shape[1:])
    total = lax.dynamic_index_in_dim(chunks, me, 0, keepdims=False)
    for k in range(1, n):
        send = lax.dynamic_index_in_dim(chunks, (me + k) % n, 0, keepdims=False)
        total = total + lax.ppermute(send, axis, shift_pairs(n, k))
    return total


def pair_all_reduce(x, axis, n):
    groups = n // 2
    if n % 2 or groups & (groups - 1):
        return lax.psum(x, axis)
    inner = lax.axis_index(axis) % 2
    halves = x.reshape(2, x.shape[0] // 2, *x.shape[1:])
    keep = lax.dynamic_index_in_dim(halves, inner, 0, keepdims=False)
    give = lax.dynamic_index_in_dim(halves, 1 - inner, 0, keepdims=False)
    part = keep + lax.ppermute(give, axis, [(i, i ^ 1) for i in range(n)])
    step = 2
    while step < n:
        pairs = [(i, i ^ step) for i in range(n)]
        pieces = jnp.split(part, 2) if part.shape[0] % 2 == 0 else [part]
        part = jnp.concatenate([p + lax.ppermute(p, axis, pairs) for p in pieces])
        step *= 2
    other = lax.ppermute(part, axis, [(i, i ^ 1) for i in range(n)])
    return jnp.roll(jnp.stack([part, other]), inner, axis=0).reshape(x.shape)


def butterfly_sum(x, axes, n):
    if n & (n - 1):
        return lax.psum(x, axes)
    step = 1
    while step < n:
        x = x + lax.ppermute(x, axes, [(i, i ^ step) for i in range(n)])
        step *= 2
    return x


def slot_product(blocks, source, block_row, block_col, counts, out_rows, transpose):
    slot_count, block_size = blocks.shape[0], blocks.shape[1]
    width = source.shape[1]
    group = 32 if slot_count % 32 == 0 else 1

    def kernel(row_ref, col_ref, count_ref, block_ref, source_ref, out_ref):
        step = pl.program_id(0)

        @pl.when(step == 0)
        def _():
            out_ref[...] = jnp.zeros_like(out_ref)

        def body(s, carry):
            slot = step * group + s
            read = row_ref[slot] if transpose else col_ref[slot]
            write = col_ref[slot] if transpose else row_ref[slot]
            read = jnp.clip(read, 0, source_ref.shape[0] // block_size - 1)
            write = jnp.clip(write, 0, out_ref.shape[0] // block_size - 1)
            live = (slot < count_ref[0]).astype(jnp.float32)
            piece = source_ref[pl.ds(pl.multiple_of(read * block_size, block_size), block_size), :]
            block = block_ref[s]
            if transpose:
                block = block.T
            product = jnp.dot(
                block, piece, precision=KERNEL_PRECISION, preferred_element_type=jnp.float32
            )
            at = pl.ds(pl.multiple_of(write * block_size, block_size), block_size)
            out_ref[at, :] = out_ref[at, :] + product * live
            return carry

        lax.fori_loop(0, group, body, 0, unroll=True)

    grid_spec = pltpu.PrefetchScalarGridSpec(
        num_scalar_prefetch=3,
        grid=(slot_count // group,),
        in_specs=[
            pl.BlockSpec((group, block_size, block_size), lambda g, *_: (g, 0, 0)),
            pl.BlockSpec(source.shape, lambda g, *_: (0, 0)),
        ],
        out_specs=pl.BlockSpec((out_rows, width), lambda g, *_: (0, 0)),
    )
    return pl.pallas_call(
        kernel,
        grid_spec=grid_spec,
        out_shape=jax.ShapeDtypeStruct((out_rows, width), jnp.float32),
        compiler_params=pltpu.CompilerParams(
            dimension_semantics=("arbitrary",), vmem_limit_bytes=48 * 1024 * 1024
        ),
        interpret=INTERPRET,
    )(block_row, block_col, counts, blocks, source)


def shards(probe, self_weight, blocks, block_row, block_col, counts):
    col_count = lax.axis_size("col")
    row_count = lax.axis_size("row")
    block_size = blocks.shape[1]
    probe_width = probe.shape[1]
    slot_count = blocks.shape[0]
    local_rows = probe.shape[0]
    owner_rows = local_rows * col_count
    owner_blocks = owner_rows // block_size
    stripe_rows = local_rows * row_count
    stripe_blocks = stripe_rows // block_size
    answers = local_rows * row_count * col_count
    stripe_probe = lax.all_gather(probe, "row", axis=0, tiled=True)
    partial_value = slot_product(
        blocks, stripe_probe, block_row, block_col, counts, owner_rows, False
    )
    local_start = lax.axis_index("col") * local_rows
    local_weight = lax.dynamic_slice_in_dim(self_weight, local_start, local_rows, 0)
    own_rows = lax.dynamic_slice_in_dim(partial_value, local_start, local_rows, 0)
    partial_value = lax.dynamic_update_slice_in_dim(
        partial_value, own_rows + local_weight[:, None] * probe, local_start, 0
    )
    owner_y = pair_all_reduce(partial_value, "col", col_count)
    projected = lax.dynamic_slice_in_dim(owner_y, local_start, local_rows, 0)
    w_partial = slot_product(blocks, owner_y, block_row, block_col, counts, stripe_rows, True)
    w_share = lax.psum_scatter(w_partial, "row", scatter_dimension=0, tiled=True)
    sketch = local_weight[:, None] * projected + w_share
    gram_part = jnp.dot(sketch.T, sketch, precision=PRECISE, preferred_element_type=jnp.float32)
    gram = butterfly_sum(gram_part, ("row", "col"), row_count * col_count)
    lower = jnp.linalg.cholesky(gram)
    lower_inverse = lax.linalg.triangular_solve(
        lower, jnp.eye(lower.shape[0], dtype=lower.dtype), left_side=True, lower=True
    )
    solved = jnp.dot(sketch, lower_inverse.T, precision=PRECISE)
    basis = solved * math.sqrt(answers)
    return (projected, basis)


def solution(mesh):
    in_specs = (
        P(("row", "col"), None),
        P("row"),
        P(("row", "col"), None, None),
        P(("row", "col")),
        P(("row", "col")),
        P(("row", "col")),
    )
    out_specs = (P(("row", "col"), None), P(("row", "col"), None))
    return jax.shard_map(shards, mesh=mesh, in_specs=in_specs, out_specs=out_specs, check_vma=False)
```

```python
import math

import jax
import jax.numpy as jnp
from jax import lax
from jax.experimental import pallas as pl
from jax.experimental.pallas import tpu as pltpu
from jax.sharding import PartitionSpec as P

PRECISE = lax.Precision.HIGHEST
INTERPRET = False
KERNEL_PRECISION = lax.Precision.HIGH


def shift_pairs(n, k):
    return [(i, (i + k) % n) for i in range(n)]


def ring_gather(x, axis, n):
    me = lax.axis_index(axis)
    parts = [x] + [lax.ppermute(x, axis, shift_pairs(n, -k)) for k in range(1, n)]
    return jnp.roll(jnp.stack(parts), me, axis=0).reshape(n * x.shape[0], *x.shape[1:])


def ring_reduce_scatter(x, axis, n):
    me = lax.axis_index(axis)
    chunks = x.reshape(n, x.shape[0] // n, *x.shape[1:])
    total = lax.dynamic_index_in_dim(chunks, me, 0, keepdims=False)
    for k in range(1, n):
        send = lax.dynamic_index_in_dim(chunks, (me + k) % n, 0, keepdims=False)
        total = total + lax.ppermute(send, axis, shift_pairs(n, k))
    return total


def pair_all_reduce(x, axis, n):
    groups = n // 2
    if n % 2 or groups & (groups - 1):
        return lax.psum(x, axis)
    inner = lax.axis_index(axis) % 2
    halves = x.reshape(2, x.shape[0] // 2, *x.shape[1:])
    keep = lax.dynamic_index_in_dim(halves, inner, 0, keepdims=False)
    give = lax.dynamic_index_in_dim(halves, 1 - inner, 0, keepdims=False)
    part = keep + lax.ppermute(give, axis, [(i, i ^ 1) for i in range(n)])
    step = 2
    while step < n:
        pairs = [(i, i ^ step) for i in range(n)]
        pieces = jnp.split(part, 2) if part.shape[0] % 2 == 0 else [part]
        part = jnp.concatenate([p + lax.ppermute(p, axis, pairs) for p in pieces])
        step *= 2
    other = lax.ppermute(part, axis, [(i, i ^ 1) for i in range(n)])
    return jnp.roll(jnp.stack([part, other]), inner, axis=0).reshape(x.shape)


def line_gather(piece, axis, n):
    groups = n // 2
    outer = lax.axis_index(axis) // 2
    up = [(i, i + 2) for i in range(n) if i + 2 < n]
    down = [(i, i - 2) for i in range(n) if i >= 2]
    from_below, from_above = piece, piece
    below, above = [], []
    for _ in range(groups - 1):
        from_below = lax.ppermute(from_below, axis, up)
        from_above = lax.ppermute(from_above, axis, down)
        below.append(from_below)
        above.append(from_above)
    line = jnp.stack(below[::-1] + [piece] + above)
    return lax.dynamic_slice_in_dim(line, groups - 1 - outer, groups, 0)


def split_route_gather(x, axis, n):
    width = x.shape[1]
    if n % 2 or width % 2:
        return lax.all_gather(x, axis, axis=0, tiled=True)
    inner = lax.axis_index(axis) % 2
    swap = [(i, i ^ 1) for i in range(n)]
    first, second = x[:, : width // 2], x[:, width // 2 :]
    pair = jnp.roll(jnp.stack([first, lax.ppermute(first, axis, swap)]), inner, axis=0)
    first_all = line_gather(pair, axis, n)
    line = line_gather(second, axis, n)
    second_all = jnp.roll(jnp.stack([line, lax.ppermute(line, axis, swap)], axis=1), inner, axis=1)
    rows = n * x.shape[0]
    return jnp.concatenate(
        [first_all.reshape(rows, width // 2), second_all.reshape(rows, width // 2)], axis=1
    )


def butterfly_sum(x, axes, n):
    if n & (n - 1):
        return lax.psum(x, axes)
    step = 1
    while step < n:
        x = x + lax.ppermute(x, axes, [(i, i ^ step) for i in range(n)])
        step *= 2
    return x


def slot_product(blocks, source, block_row, block_col, counts, out_rows, transpose):
    slot_count, block_size = blocks.shape[0], blocks.shape[1]
    width = source.shape[1]
    group = 32 if slot_count % 32 == 0 else 1

    def kernel(row_ref, col_ref, count_ref, block_ref, source_ref, out_ref):
        step = pl.program_id(0)

        @pl.when(step == 0)
        def _():
            out_ref[...] = jnp.zeros_like(out_ref)

        def body(s, carry):
            slot = step * group + s
            read = row_ref[slot] if transpose else col_ref[slot]
            write = col_ref[slot] if transpose else row_ref[slot]
            read = jnp.clip(read, 0, source_ref.shape[0] // block_size - 1)
            write = jnp.clip(write, 0, out_ref.shape[0] // block_size - 1)
            live = (slot < count_ref[0]).astype(jnp.float32)
            piece = source_ref[pl.ds(pl.multiple_of(read * block_size, block_size), block_size), :]
            block = block_ref[s]
            if transpose:
                block = block.T
            product = jnp.dot(
                block, piece, precision=KERNEL_PRECISION, preferred_element_type=jnp.float32
            )
            at = pl.ds(pl.multiple_of(write * block_size, block_size), block_size)
            out_ref[at, :] = out_ref[at, :] + product * live
            return carry

        lax.fori_loop(0, group, body, 0, unroll=True)

    grid_spec = pltpu.PrefetchScalarGridSpec(
        num_scalar_prefetch=3,
        grid=(slot_count // group,),
        in_specs=[
            pl.BlockSpec((group, block_size, block_size), lambda g, *_: (g, 0, 0)),
            pl.BlockSpec(source.shape, lambda g, *_: (0, 0)),
        ],
        out_specs=pl.BlockSpec((out_rows, width), lambda g, *_: (0, 0)),
    )
    return pl.pallas_call(
        kernel,
        grid_spec=grid_spec,
        out_shape=jax.ShapeDtypeStruct((out_rows, width), jnp.float32),
        compiler_params=pltpu.CompilerParams(
            dimension_semantics=("arbitrary",), vmem_limit_bytes=48 * 1024 * 1024
        ),
        interpret=INTERPRET,
    )(block_row, block_col, counts, blocks, source)


def shards(probe, self_weight, blocks, block_row, block_col, counts):
    col_count = lax.axis_size("col")
    row_count = lax.axis_size("row")
    block_size = blocks.shape[1]
    probe_width = probe.shape[1]
    slot_count = blocks.shape[0]
    local_rows = probe.shape[0]
    owner_rows = local_rows * col_count
    owner_blocks = owner_rows // block_size
    stripe_rows = local_rows * row_count
    stripe_blocks = stripe_rows // block_size
    answers = local_rows * row_count * col_count
    stripe_probe = split_route_gather(probe, "row", row_count)
    partial_value = slot_product(
        blocks, stripe_probe, block_row, block_col, counts, owner_rows, False
    )
    local_start = lax.axis_index("col") * local_rows
    local_weight = lax.dynamic_slice_in_dim(self_weight, local_start, local_rows, 0)
    own_rows = lax.dynamic_slice_in_dim(partial_value, local_start, local_rows, 0)
    partial_value = lax.dynamic_update_slice_in_dim(
        partial_value, own_rows + local_weight[:, None] * probe, local_start, 0
    )
    owner_y = pair_all_reduce(partial_value, "col", col_count)
    projected = lax.dynamic_slice_in_dim(owner_y, local_start, local_rows, 0)
    w_partial = slot_product(blocks, owner_y, block_row, block_col, counts, stripe_rows, True)
    w_share = lax.psum_scatter(w_partial, "row", scatter_dimension=0, tiled=True)
    sketch = local_weight[:, None] * projected + w_share
    gram_part = jnp.dot(sketch.T, sketch, precision=PRECISE, preferred_element_type=jnp.float32)
    gram = butterfly_sum(gram_part, ("row", "col"), row_count * col_count)
    lower = jnp.linalg.cholesky(gram)
    lower_inverse = lax.linalg.triangular_solve(
        lower, jnp.eye(lower.shape[0], dtype=lower.dtype), left_side=True, lower=True
    )
    solved = jnp.dot(sketch, lower_inverse.T, precision=PRECISE)
    basis = solved * math.sqrt(answers)
    return (projected, basis)


def solution(mesh):
    in_specs = (
        P(("row", "col"), None),
        P("row"),
        P(("row", "col"), None, None),
        P(("row", "col")),
        P(("row", "col")),
        P(("row", "col")),
    )
    out_specs = (P(("row", "col"), None), P(("row", "col"), None))
    return jax.shard_map(shards, mesh=mesh, in_specs=in_specs, out_specs=out_specs, check_vma=False)
```

```python
import math

import jax
import jax.numpy as jnp
from jax import lax
from jax.experimental import pallas as pl
from jax.experimental.pallas import tpu as pltpu
from jax.sharding import PartitionSpec as P

PRECISE = lax.Precision.HIGHEST
INTERPRET = False
KERNEL_PRECISION = lax.Precision.HIGH
ACCUMULATORS = 4


def shift_pairs(n, k):
    return [(i, (i + k) % n) for i in range(n)]


def ring_gather(x, axis, n):
    me = lax.axis_index(axis)
    parts = [x] + [lax.ppermute(x, axis, shift_pairs(n, -k)) for k in range(1, n)]
    return jnp.roll(jnp.stack(parts), me, axis=0).reshape(n * x.shape[0], *x.shape[1:])


def ring_reduce_scatter(x, axis, n):
    me = lax.axis_index(axis)
    chunks = x.reshape(n, x.shape[0] // n, *x.shape[1:])
    total = lax.dynamic_index_in_dim(chunks, me, 0, keepdims=False)
    for k in range(1, n):
        send = lax.dynamic_index_in_dim(chunks, (me + k) % n, 0, keepdims=False)
        total = total + lax.ppermute(send, axis, shift_pairs(n, k))
    return total


def pair_all_reduce(x, axis, n):
    groups = n // 2
    if n % 2 or groups & (groups - 1):
        return lax.psum(x, axis)
    inner = lax.axis_index(axis) % 2
    halves = x.reshape(2, x.shape[0] // 2, *x.shape[1:])
    keep = lax.dynamic_index_in_dim(halves, inner, 0, keepdims=False)
    give = lax.dynamic_index_in_dim(halves, 1 - inner, 0, keepdims=False)
    part = keep + lax.ppermute(give, axis, [(i, i ^ 1) for i in range(n)])
    step = 2
    while step < n:
        part = part + lax.ppermute(part, axis, [(i, i ^ step) for i in range(n)])
        step *= 2
    other = lax.ppermute(part, axis, [(i, i ^ 1) for i in range(n)])
    return jnp.roll(jnp.stack([part, other]), inner, axis=0).reshape(x.shape)


def butterfly_sum(x, axes, n):
    if n & (n - 1):
        return lax.psum(x, axes)
    step = 1
    while step < n:
        x = x + lax.ppermute(x, axes, [(i, i ^ step) for i in range(n)])
        step *= 2
    return x


def slot_product(blocks, source, block_row, block_col, counts, out_rows, transpose):
    slot_count, block_size = blocks.shape[0], blocks.shape[1]
    width = source.shape[1]
    group = 32 if slot_count % 32 == 0 else 1
    lanes = ACCUMULATORS if group % ACCUMULATORS == 0 else 1

    def kernel(row_ref, col_ref, count_ref, block_ref, source_ref, out_ref, *sums):
        step = pl.program_id(0)

        @pl.when(step == 0)
        def _():
            for acc in sums:
                acc[...] = jnp.zeros_like(acc)

        def body(t, carry):
            for lane in range(lanes):
                s = t * lanes + lane
                slot = step * group + s
                read = row_ref[slot] if transpose else col_ref[slot]
                write = col_ref[slot] if transpose else row_ref[slot]
                read = jnp.clip(read, 0, source_ref.shape[0] // block_size - 1)
                write = jnp.clip(write, 0, out_ref.shape[0] // block_size - 1)
                live = (slot < count_ref[0]).astype(jnp.float32)
                at_read = pl.ds(pl.multiple_of(read * block_size, block_size), block_size)
                piece = source_ref[at_read, :]
                block = block_ref[s]
                if transpose:
                    block = block.T
                product = jnp.dot(
                    block, piece, precision=KERNEL_PRECISION, preferred_element_type=jnp.float32
                )
                at = pl.ds(pl.multiple_of(write * block_size, block_size), block_size)
                acc = sums[lane]
                acc[at, :] = acc[at, :] + product * live
            return carry

        lax.fori_loop(0, group // lanes, body, 0, unroll=True)

        @pl.when(step == pl.num_programs(0) - 1)
        def _():
            total = sums[0][...]
            for acc in sums[1:]:
                total = total + acc[...]
            out_ref[...] = total

    grid_spec = pltpu.PrefetchScalarGridSpec(
        num_scalar_prefetch=3,
        grid=(slot_count // group,),
        in_specs=[
            pl.BlockSpec((group, block_size, block_size), lambda g, *_: (g, 0, 0)),
            pl.BlockSpec(source.shape, lambda g, *_: (0, 0)),
        ],
        out_specs=pl.BlockSpec((out_rows, width), lambda g, *_: (0, 0)),
        scratch_shapes=[pltpu.VMEM((out_rows, width), jnp.float32) for _ in range(lanes)],
    )
    return pl.pallas_call(
        kernel,
        grid_spec=grid_spec,
        out_shape=jax.ShapeDtypeStruct((out_rows, width), jnp.float32),
        compiler_params=pltpu.CompilerParams(
            dimension_semantics=("arbitrary",), vmem_limit_bytes=56 * 1024 * 1024
        ),
        interpret=INTERPRET,
    )(block_row, block_col, counts, blocks, source)


def shards(probe, self_weight, blocks, block_row, block_col, counts):
    col_count = lax.axis_size("col")
    row_count = lax.axis_size("row")
    block_size = blocks.shape[1]
    probe_width = probe.shape[1]
    slot_count = blocks.shape[0]
    local_rows = probe.shape[0]
    owner_rows = local_rows * col_count
    owner_blocks = owner_rows // block_size
    stripe_rows = local_rows * row_count
    stripe_blocks = stripe_rows // block_size
    answers = local_rows * row_count * col_count
    stripe_probe = lax.all_gather(probe, "row", axis=0, tiled=True)
    partial_value = slot_product(
        blocks, stripe_probe, block_row, block_col, counts, owner_rows, False
    )
    local_start = lax.axis_index("col") * local_rows
    local_weight = lax.dynamic_slice_in_dim(self_weight, local_start, local_rows, 0)
    own_rows = lax.dynamic_slice_in_dim(partial_value, local_start, local_rows, 0)
    partial_value = lax.dynamic_update_slice_in_dim(
        partial_value, own_rows + local_weight[:, None] * probe, local_start, 0
    )
    owner_y = pair_all_reduce(partial_value, "col", col_count)
    projected = lax.dynamic_slice_in_dim(owner_y, local_start, local_rows, 0)
    w_partial = slot_product(blocks, owner_y, block_row, block_col, counts, stripe_rows, True)
    w_share = lax.psum_scatter(w_partial, "row", scatter_dimension=0, tiled=True)
    sketch = local_weight[:, None] * projected + w_share
    gram_part = jnp.dot(sketch.T, sketch, precision=PRECISE, preferred_element_type=jnp.float32)
    gram = butterfly_sum(gram_part, ("row", "col"), row_count * col_count)
    lower = jnp.linalg.cholesky(gram)
    solved = lax.linalg.triangular_solve(
        lower, sketch, left_side=False, lower=True, transpose_a=True
    )
    basis = solved * math.sqrt(answers)
    return (projected, basis)


def solution(mesh):
    in_specs = (
        P(("row", "col"), None),
        P("row"),
        P(("row", "col"), None, None),
        P(("row", "col")),
        P(("row", "col")),
        P(("row", "col")),
    )
    out_specs = (P(("row", "col"), None), P(("row", "col"), None))
    return jax.shard_map(shards, mesh=mesh, in_specs=in_specs, out_specs=out_specs, check_vma=False)
```

```python
import math

import jax
import jax.numpy as jnp
from jax import lax
from jax.experimental import pallas as pl
from jax.experimental.pallas import tpu as pltpu
from jax.sharding import PartitionSpec as P

PRECISE = lax.Precision.HIGHEST
INTERPRET = False
KERNEL_PRECISION = lax.Precision.HIGH


def shift_pairs(n, k):
    return [(i, (i + k) % n) for i in range(n)]


def ring_gather(x, axis, n):
    me = lax.axis_index(axis)
    parts = [x] + [lax.ppermute(x, axis, shift_pairs(n, -k)) for k in range(1, n)]
    return jnp.roll(jnp.stack(parts), me, axis=0).reshape(n * x.shape[0], *x.shape[1:])


def ring_reduce_scatter(x, axis, n):
    me = lax.axis_index(axis)
    chunks = x.reshape(n, x.shape[0] // n, *x.shape[1:])
    total = lax.dynamic_index_in_dim(chunks, me, 0, keepdims=False)
    for k in range(1, n):
        send = lax.dynamic_index_in_dim(chunks, (me + k) % n, 0, keepdims=False)
        total = total + lax.ppermute(send, axis, shift_pairs(n, k))
    return total


def pair_all_reduce(x, axis, n):
    groups = n // 2
    if n % 2 or groups & (groups - 1):
        return lax.psum(x, axis)
    inner = lax.axis_index(axis) % 2
    halves = x.reshape(2, x.shape[0] // 2, *x.shape[1:])
    keep = lax.dynamic_index_in_dim(halves, inner, 0, keepdims=False)
    give = lax.dynamic_index_in_dim(halves, 1 - inner, 0, keepdims=False)
    part = keep + lax.ppermute(give, axis, [(i, i ^ 1) for i in range(n)])
    step = 2
    while step < n:
        part = part + lax.ppermute(part, axis, [(i, i ^ step) for i in range(n)])
        step *= 2
    other = lax.ppermute(part, axis, [(i, i ^ 1) for i in range(n)])
    return jnp.roll(jnp.stack([part, other]), inner, axis=0).reshape(x.shape)


def butterfly_sum(x, axes, n):
    if n & (n - 1):
        return lax.psum(x, axes)
    step = 1
    while step < n:
        x = x + lax.ppermute(x, axes, [(i, i ^ step) for i in range(n)])
        step *= 2
    return x


def slot_product(blocks, source, block_row, block_col, counts, out_rows, transpose):
    slot_count, block_size = blocks.shape[0], blocks.shape[1]
    width = source.shape[1]
    group = 16 if slot_count % 16 == 0 else 1

    def kernel(row_ref, col_ref, count_ref, block_ref, source_ref, out_ref):
        step = pl.program_id(0)

        @pl.when(step == 0)
        def _():
            out_ref[...] = jnp.zeros_like(out_ref)

        def body(s, carry):
            slot = step * group + s
            read = row_ref[slot] if transpose else col_ref[slot]
            write = col_ref[slot] if transpose else row_ref[slot]
            read = jnp.clip(read, 0, source_ref.shape[0] // block_size - 1)
            write = jnp.clip(write, 0, out_ref.shape[0] // block_size - 1)
            live = (slot < count_ref[0]).astype(jnp.float32)
            piece = source_ref[pl.ds(pl.multiple_of(read * block_size, block_size), block_size), :]
            block = block_ref[s]
            if transpose:
                block = block.T
            product = jnp.dot(
                block, piece, precision=KERNEL_PRECISION, preferred_element_type=jnp.float32
            )
            at = pl.ds(pl.multiple_of(write * block_size, block_size), block_size)
            out_ref[at, :] = out_ref[at, :] + product * live
            return carry

        lax.fori_loop(0, group, body, 0, unroll=True)

    grid_spec = pltpu.PrefetchScalarGridSpec(
        num_scalar_prefetch=3,
        grid=(slot_count // group,),
        in_specs=[
            pl.BlockSpec((group, block_size, block_size), lambda g, *_: (g, 0, 0)),
            pl.BlockSpec(source.shape, lambda g, *_: (0, 0)),
        ],
        out_specs=pl.BlockSpec((out_rows, width), lambda g, *_: (0, 0)),
    )
    return pl.pallas_call(
        kernel,
        grid_spec=grid_spec,
        out_shape=jax.ShapeDtypeStruct((out_rows, width), jnp.float32),
        compiler_params=pltpu.CompilerParams(
            dimension_semantics=("arbitrary",), vmem_limit_bytes=48 * 1024 * 1024
        ),
        interpret=INTERPRET,
    )(block_row, block_col, counts, blocks, source)


def shards(probe, self_weight, blocks, block_row, block_col, counts):
    col_count = lax.axis_size("col")
    row_count = lax.axis_size("row")
    block_size = blocks.shape[1]
    probe_width = probe.shape[1]
    slot_count = blocks.shape[0]
    local_rows = probe.shape[0]
    owner_rows = local_rows * col_count
    owner_blocks = owner_rows // block_size
    stripe_rows = local_rows * row_count
    stripe_blocks = stripe_rows // block_size
    answers = local_rows * row_count * col_count
    stripe_probe = lax.all_gather(probe, "row", axis=0, tiled=True)
    partial_value = slot_product(
        blocks, stripe_probe, block_row, block_col, counts, owner_rows, False
    )
    local_start = lax.axis_index("col") * local_rows
    local_weight = lax.dynamic_slice_in_dim(self_weight, local_start, local_rows, 0)
    own_rows = lax.dynamic_slice_in_dim(partial_value, local_start, local_rows, 0)
    partial_value = lax.dynamic_update_slice_in_dim(
        partial_value, own_rows + local_weight[:, None] * probe, local_start, 0
    )
    owner_y = pair_all_reduce(partial_value, "col", col_count)
    projected = lax.dynamic_slice_in_dim(owner_y, local_start, local_rows, 0)
    w_partial = slot_product(blocks, owner_y, block_row, block_col, counts, stripe_rows, True)
    w_share = lax.psum_scatter(w_partial, "row", scatter_dimension=0, tiled=True)
    sketch = local_weight[:, None] * projected + w_share
    gram_part = jnp.dot(sketch.T, sketch, precision=PRECISE, preferred_element_type=jnp.float32)
    gram = butterfly_sum(gram_part, ("row", "col"), row_count * col_count)
    lower = lax.linalg.cholesky(gram, symmetrize_input=False)
    solved = lax.linalg.triangular_solve(
        lower, sketch, left_side=False, lower=True, transpose_a=True
    )
    basis = solved * math.sqrt(answers)
    return (projected, basis)


def solution(mesh):
    in_specs = (
        P(("row", "col"), None),
        P("row"),
        P(("row", "col"), None, None),
        P(("row", "col")),
        P(("row", "col")),
        P(("row", "col")),
    )
    out_specs = (P(("row", "col"), None), P(("row", "col"), None))
    return jax.shard_map(shards, mesh=mesh, in_specs=in_specs, out_specs=out_specs, check_vma=False)
```

```python
import math

import jax
import jax.numpy as jnp
from jax import lax
from jax.experimental import pallas as pl
from jax.experimental.pallas import tpu as pltpu
from jax.sharding import PartitionSpec as P

PRECISE = lax.Precision.HIGHEST
INTERPRET = False
KERNEL_PRECISION = lax.Precision.HIGH


def shift_pairs(n, k):
    return [(i, (i + k) % n) for i in range(n)]


def ring_gather(x, axis, n):
    me = lax.axis_index(axis)
    parts = [x] + [lax.ppermute(x, axis, shift_pairs(n, -k)) for k in range(1, n)]
    return jnp.roll(jnp.stack(parts), me, axis=0).reshape(n * x.shape[0], *x.shape[1:])


def ring_reduce_scatter(x, axis, n):
    me = lax.axis_index(axis)
    chunks = x.reshape(n, x.shape[0] // n, *x.shape[1:])
    total = lax.dynamic_index_in_dim(chunks, me, 0, keepdims=False)
    for k in range(1, n):
        send = lax.dynamic_index_in_dim(chunks, (me + k) % n, 0, keepdims=False)
        total = total + lax.ppermute(send, axis, shift_pairs(n, k))
    return total


def pair_all_reduce(x, axis, n):
    groups = n // 2
    if n % 2 or groups & (groups - 1):
        return lax.psum(x, axis)
    inner = lax.axis_index(axis) % 2
    halves = x.reshape(2, x.shape[0] // 2, *x.shape[1:])
    keep = lax.dynamic_index_in_dim(halves, inner, 0, keepdims=False)
    give = lax.dynamic_index_in_dim(halves, 1 - inner, 0, keepdims=False)
    part = keep + lax.ppermute(give, axis, [(i, i ^ 1) for i in range(n)])
    step = 2
    while step < n:
        part = part + lax.ppermute(part, axis, [(i, i ^ step) for i in range(n)])
        step *= 2
    other = lax.ppermute(part, axis, [(i, i ^ 1) for i in range(n)])
    return jnp.roll(jnp.stack([part, other]), inner, axis=0).reshape(x.shape)


def butterfly_sum(x, axes, n):
    if n & (n - 1):
        return lax.psum(x, axes)
    step = 1
    while step < n:
        x = x + lax.ppermute(x, axes, [(i, i ^ step) for i in range(n)])
        step *= 2
    return x


def slot_product(blocks, source, block_row, block_col, counts, out_rows, transpose):
    slot_count, block_size = blocks.shape[0], blocks.shape[1]
    width = source.shape[1]
    group = 64 if slot_count % 64 == 0 else 1

    def kernel(row_ref, col_ref, count_ref, block_ref, source_ref, out_ref):
        step = pl.program_id(0)

        @pl.when(step == 0)
        def _():
            out_ref[...] = jnp.zeros_like(out_ref)

        def body(s, carry):
            slot = step * group + s
            read = row_ref[slot] if transpose else col_ref[slot]
            write = col_ref[slot] if transpose else row_ref[slot]
            read = jnp.clip(read, 0, source_ref.shape[0] // block_size - 1)
            write = jnp.clip(write, 0, out_ref.shape[0] // block_size - 1)
            live = (slot < count_ref[0]).astype(jnp.float32)
            piece = source_ref[pl.ds(pl.multiple_of(read * block_size, block_size), block_size), :]
            block = block_ref[s]
            if transpose:
                block = block.T
            product = jnp.dot(
                block, piece, precision=KERNEL_PRECISION, preferred_element_type=jnp.float32
            )
            at = pl.ds(pl.multiple_of(write * block_size, block_size), block_size)
            out_ref[at, :] = out_ref[at, :] + product * live
            return carry

        lax.fori_loop(0, group, body, 0, unroll=True)

    grid_spec = pltpu.PrefetchScalarGridSpec(
        num_scalar_prefetch=3,
        grid=(slot_count // group,),
        in_specs=[
            pl.BlockSpec((group, block_size, block_size), lambda g, *_: (g, 0, 0)),
            pl.BlockSpec(source.shape, lambda g, *_: (0, 0)),
        ],
        out_specs=pl.BlockSpec((out_rows, width), lambda g, *_: (0, 0)),
    )
    return pl.pallas_call(
        kernel,
        grid_spec=grid_spec,
        out_shape=jax.ShapeDtypeStruct((out_rows, width), jnp.float32),
        compiler_params=pltpu.CompilerParams(
            dimension_semantics=("arbitrary",), vmem_limit_bytes=48 * 1024 * 1024
        ),
        interpret=INTERPRET,
    )(block_row, block_col, counts, blocks, source)


def shards(probe, self_weight, blocks, block_row, block_col, counts):
    col_count = lax.axis_size("col")
    row_count = lax.axis_size("row")
    block_size = blocks.shape[1]
    probe_width = probe.shape[1]
    slot_count = blocks.shape[0]
    local_rows = probe.shape[0]
    owner_rows = local_rows * col_count
    owner_blocks = owner_rows // block_size
    stripe_rows = local_rows * row_count
    stripe_blocks = stripe_rows // block_size
    answers = local_rows * row_count * col_count
    stripe_probe = lax.all_gather(probe, "row", axis=0, tiled=True)
    partial_value = slot_product(
        blocks, stripe_probe, block_row, block_col, counts, owner_rows, False
    )
    local_start = lax.axis_index("col") * local_rows
    local_weight = lax.dynamic_slice_in_dim(self_weight, local_start, local_rows, 0)
    own_rows = lax.dynamic_slice_in_dim(partial_value, local_start, local_rows, 0)
    partial_value = lax.dynamic_update_slice_in_dim(
        partial_value, own_rows + local_weight[:, None] * probe, local_start, 0
    )
    owner_y = pair_all_reduce(partial_value, "col", col_count)
    projected = lax.dynamic_slice_in_dim(owner_y, local_start, local_rows, 0)
    w_partial = slot_product(blocks, owner_y, block_row, block_col, counts, stripe_rows, True)
    w_share = lax.psum_scatter(w_partial, "row", scatter_dimension=0, tiled=True)
    sketch = local_weight[:, None] * projected + w_share
    gram_part = jnp.dot(sketch.T, sketch, precision=PRECISE, preferred_element_type=jnp.float32)
    gram = butterfly_sum(gram_part, ("row", "col"), row_count * col_count)
    lower = jnp.linalg.cholesky(gram)
    solved = lax.linalg.triangular_solve(
        lower, sketch, left_side=False, lower=True, transpose_a=True
    )
    basis = solved * math.sqrt(answers)
    return (projected, basis)


def solution(mesh):
    in_specs = (
        P(("row", "col"), None),
        P("row"),
        P(("row", "col"), None, None),
        P(("row", "col")),
        P(("row", "col")),
        P(("row", "col")),
    )
    out_specs = (P(("row", "col"), None), P(("row", "col"), None))
    return jax.shard_map(shards, mesh=mesh, in_specs=in_specs, out_specs=out_specs, check_vma=False)
```

```python
import math

import jax
import jax.numpy as jnp
from jax import lax
from jax.experimental import pallas as pl
from jax.experimental.pallas import tpu as pltpu
from jax.sharding import PartitionSpec as P

PRECISE = lax.Precision.HIGHEST
INTERPRET = False
KERNEL_PRECISION = lax.Precision.HIGH


def shift_pairs(n, k):
    return [(i, (i + k) % n) for i in range(n)]


def ring_gather(x, axis, n):
    me = lax.axis_index(axis)
    parts = [x] + [lax.ppermute(x, axis, shift_pairs(n, -k)) for k in range(1, n)]
    return jnp.roll(jnp.stack(parts), me, axis=0).reshape(n * x.shape[0], *x.shape[1:])


def ring_reduce_scatter(x, axis, n):
    me = lax.axis_index(axis)
    chunks = x.reshape(n, x.shape[0] // n, *x.shape[1:])
    total = lax.dynamic_index_in_dim(chunks, me, 0, keepdims=False)
    for k in range(1, n):
        send = lax.dynamic_index_in_dim(chunks, (me + k) % n, 0, keepdims=False)
        total = total + lax.ppermute(send, axis, shift_pairs(n, k))
    return total


def pair_all_reduce(x, axis, n):
    groups = n // 2
    if n % 2 or groups & (groups - 1):
        return lax.psum(x, axis), None, 0
    inner = lax.axis_index(axis) % 2
    halves = x.reshape(2, x.shape[0] // 2, *x.shape[1:])
    keep = lax.dynamic_index_in_dim(halves, inner, 0, keepdims=False)
    give = lax.dynamic_index_in_dim(halves, 1 - inner, 0, keepdims=False)
    part = keep + lax.ppermute(give, axis, [(i, i ^ 1) for i in range(n)])
    step = 2
    while step < n:
        part = part + lax.ppermute(part, axis, [(i, i ^ step) for i in range(n)])
        step *= 2
    other = lax.ppermute(part, axis, [(i, i ^ 1) for i in range(n)])
    return part, other, inner


def butterfly_sum(x, axes, n):
    if n & (n - 1):
        return lax.psum(x, axes)
    step = 1
    while step < n:
        x = x + lax.ppermute(x, axes, [(i, i ^ step) for i in range(n)])
        step *= 2
    return x


def slot_product(blocks, sources, inner, block_row, block_col, counts, out_rows, transpose):
    slot_count, block_size = blocks.shape[0], blocks.shape[1]
    width = sources[0].shape[1]
    half_blocks = sources[0].shape[0] // block_size
    total_blocks = half_blocks * len(sources)
    group = 32 if slot_count % 32 == 0 else 1

    def kernel(row_ref, col_ref, count_ref, inner_ref, block_ref, *refs):
        out_ref = refs[-1]
        source_refs = refs[:-1]
        step = pl.program_id(0)

        @pl.when(step == 0)
        def _():
            out_ref[...] = jnp.zeros_like(out_ref)

        def body(s, carry):
            slot = step * group + s
            read = row_ref[slot] if transpose else col_ref[slot]
            write = col_ref[slot] if transpose else row_ref[slot]
            read = jnp.clip(read, 0, total_blocks - 1)
            write = jnp.clip(write, 0, out_ref.shape[0] // block_size - 1)
            live = (slot < count_ref[0]).astype(jnp.float32)
            local = read % half_blocks
            at_read = pl.ds(pl.multiple_of(local * block_size, block_size), block_size)
            piece = source_refs[0][at_read, :]
            if len(source_refs) > 1:
                piece = jnp.where(read // half_blocks == inner_ref[0], piece, source_refs[1][at_read, :])
            block = block_ref[s]
            if transpose:
                block = block.T
            product = jnp.dot(
                block, piece, precision=KERNEL_PRECISION, preferred_element_type=jnp.float32
            )
            at = pl.ds(pl.multiple_of(write * block_size, block_size), block_size)
            out_ref[at, :] = out_ref[at, :] + product * live
            return carry

        lax.fori_loop(0, group, body, 0, unroll=True)

    grid_spec = pltpu.PrefetchScalarGridSpec(
        num_scalar_prefetch=4,
        grid=(slot_count // group,),
        in_specs=[
            pl.BlockSpec((group, block_size, block_size), lambda g, *_: (g, 0, 0)),
        ]
        + [pl.BlockSpec(source.shape, lambda g, *_: (0, 0)) for source in sources],
        out_specs=pl.BlockSpec((out_rows, width), lambda g, *_: (0, 0)),
    )
    return pl.pallas_call(
        kernel,
        grid_spec=grid_spec,
        out_shape=jax.ShapeDtypeStruct((out_rows, width), jnp.float32),
        compiler_params=pltpu.CompilerParams(
            dimension_semantics=("arbitrary",), vmem_limit_bytes=48 * 1024 * 1024
        ),
        interpret=INTERPRET,
    )(block_row, block_col, counts, inner, blocks, *sources)


def shards(probe, self_weight, blocks, block_row, block_col, counts):
    col_count = lax.axis_size("col")
    row_count = lax.axis_size("row")
    block_size = blocks.shape[1]
    probe_width = probe.shape[1]
    slot_count = blocks.shape[0]
    local_rows = probe.shape[0]
    owner_rows = local_rows * col_count
    owner_blocks = owner_rows // block_size
    stripe_rows = local_rows * row_count
    stripe_blocks = stripe_rows // block_size
    answers = local_rows * row_count * col_count
    stripe_probe = lax.all_gather(probe, "row", axis=0, tiled=True)
    partial_value = slot_product(
        blocks, (stripe_probe,), jnp.zeros((1,), jnp.int32), block_row, block_col, counts,
        owner_rows, False,
    )
    local_start = lax.axis_index("col") * local_rows
    local_weight = lax.dynamic_slice_in_dim(self_weight, local_start, local_rows, 0)
    own_rows = lax.dynamic_slice_in_dim(partial_value, local_start, local_rows, 0)
    partial_value = lax.dynamic_update_slice_in_dim(
        partial_value, own_rows + local_weight[:, None] * probe, local_start, 0
    )
    part, other, inner = pair_all_reduce(partial_value, "col", col_count)
    inner = jnp.reshape(inner, (1,)).astype(jnp.int32)
    if other is None:
        sources = (part,)
        projected = lax.dynamic_slice_in_dim(part, local_start, local_rows, 0)
    else:
        sources = (part, other)
        half_rows = part.shape[0]
        offset = local_start % half_rows
        projected = jnp.where(
            local_start // half_rows == inner[0],
            lax.dynamic_slice_in_dim(part, offset, local_rows, 0),
            lax.dynamic_slice_in_dim(other, offset, local_rows, 0),
        )
    w_partial = slot_product(
        blocks, sources, inner, block_row, block_col, counts, stripe_rows, True
    )
    w_share = lax.psum_scatter(w_partial, "row", scatter_dimension=0, tiled=True)
    sketch = local_weight[:, None] * projected + w_share
    gram_part = jnp.dot(sketch.T, sketch, precision=PRECISE, preferred_element_type=jnp.float32)
    gram = butterfly_sum(gram_part, ("row", "col"), row_count * col_count)
    lower = jnp.linalg.cholesky(gram)
    solved = lax.linalg.triangular_solve(
        lower, sketch, left_side=False, lower=True, transpose_a=True
    )
    basis = solved * math.sqrt(answers)
    return (projected, basis)


def solution(mesh):
    in_specs = (
        P(("row", "col"), None),
        P("row"),
        P(("row", "col"), None, None),
        P(("row", "col")),
        P(("row", "col")),
        P(("row", "col")),
    )
    out_specs = (P(("row", "col"), None), P(("row", "col"), None))
    return jax.shard_map(shards, mesh=mesh, in_specs=in_specs, out_specs=out_specs, check_vma=False)
```

```python
import math

import jax
import jax.numpy as jnp
from jax import lax
from jax.experimental import pallas as pl
from jax.experimental.pallas import tpu as pltpu
from jax.sharding import PartitionSpec as P

PRECISE = lax.Precision.HIGHEST
INTERPRET = False
KERNEL_PRECISION = lax.Precision.HIGH


def shift_pairs(n, k):
    return [(i, (i + k) % n) for i in range(n)]


def ring_gather(x, axis, n):
    me = lax.axis_index(axis)
    parts = [x] + [lax.ppermute(x, axis, shift_pairs(n, -k)) for k in range(1, n)]
    return jnp.roll(jnp.stack(parts), me, axis=0).reshape(n * x.shape[0], *x.shape[1:])


def ring_reduce_scatter(x, axis, n):
    me = lax.axis_index(axis)
    chunks = x.reshape(n, x.shape[0] // n, *x.shape[1:])
    total = lax.dynamic_index_in_dim(chunks, me, 0, keepdims=False)
    for k in range(1, n):
        send = lax.dynamic_index_in_dim(chunks, (me + k) % n, 0, keepdims=False)
        total = total + lax.ppermute(send, axis, shift_pairs(n, k))
    return total


def pair_all_reduce(x, axis, n):
    groups = n // 2
    if n % 2 or groups & (groups - 1):
        return lax.psum(x, axis), None, 0
    inner = lax.axis_index(axis) % 2
    halves = x.reshape(2, x.shape[0] // 2, *x.shape[1:])
    keep = lax.dynamic_index_in_dim(halves, inner, 0, keepdims=False)
    give = lax.dynamic_index_in_dim(halves, 1 - inner, 0, keepdims=False)
    part = keep + lax.ppermute(give, axis, [(i, i ^ 1) for i in range(n)])
    step = 2
    while step < n:
        part = part + lax.ppermute(part, axis, [(i, i ^ step) for i in range(n)])
        step *= 2
    other = lax.ppermute(part, axis, [(i, i ^ 1) for i in range(n)])
    return part, other, inner


def butterfly_sum(x, axes, n):
    if n & (n - 1):
        return lax.psum(x, axes)
    step = 1
    while step < n:
        x = x + lax.ppermute(x, axes, [(i, i ^ step) for i in range(n)])
        step *= 2
    return x


def slot_product(blocks, sources, inner, block_row, block_col, counts, out_rows, transpose):
    slot_count, block_size = blocks.shape[0], blocks.shape[1]
    width = sources[0].shape[1]
    half_blocks = sources[0].shape[0] // block_size
    total_blocks = half_blocks * len(sources)
    group = 64 if slot_count % 64 == 0 else 1

    def kernel(row_ref, col_ref, count_ref, inner_ref, block_ref, *refs):
        out_ref = refs[-1]
        source_refs = refs[:-1]
        step = pl.program_id(0)

        @pl.when(step == 0)
        def _():
            out_ref[...] = jnp.zeros_like(out_ref)

        def body(s, carry):
            slot = step * group + s
            read = row_ref[slot] if transpose else col_ref[slot]
            write = col_ref[slot] if transpose else row_ref[slot]
            read = jnp.clip(read, 0, total_blocks - 1)
            write = jnp.clip(write, 0, out_ref.shape[0] // block_size - 1)
            live = (slot < count_ref[0]).astype(jnp.float32)
            local = read % half_blocks
            at_read = pl.ds(pl.multiple_of(local * block_size, block_size), block_size)
            piece = source_refs[0][at_read, :]
            if len(source_refs) > 1:
                piece = jnp.where(read // half_blocks == inner_ref[0], piece, source_refs[1][at_read, :])
            block = block_ref[s]
            if transpose:
                block = block.T
            product = jnp.dot(
                block, piece, precision=KERNEL_PRECISION, preferred_element_type=jnp.float32
            )
            at = pl.ds(pl.multiple_of(write * block_size, block_size), block_size)
            out_ref[at, :] = out_ref[at, :] + product * live
            return carry

        lax.fori_loop(0, group, body, 0, unroll=True)

    grid_spec = pltpu.PrefetchScalarGridSpec(
        num_scalar_prefetch=4,
        grid=(slot_count // group,),
        in_specs=[
            pl.BlockSpec((group, block_size, block_size), lambda g, *_: (g, 0, 0)),
        ]
        + [pl.BlockSpec(source.shape, lambda g, *_: (0, 0)) for source in sources],
        out_specs=pl.BlockSpec((out_rows, width), lambda g, *_: (0, 0)),
    )
    return pl.pallas_call(
        kernel,
        grid_spec=grid_spec,
        out_shape=jax.ShapeDtypeStruct((out_rows, width), jnp.float32),
        compiler_params=pltpu.CompilerParams(
            dimension_semantics=("arbitrary",), vmem_limit_bytes=48 * 1024 * 1024
        ),
        interpret=INTERPRET,
    )(block_row, block_col, counts, inner, blocks, *sources)


def shards(probe, self_weight, blocks, block_row, block_col, counts):
    col_count = lax.axis_size("col")
    row_count = lax.axis_size("row")
    block_size = blocks.shape[1]
    probe_width = probe.shape[1]
    slot_count = blocks.shape[0]
    local_rows = probe.shape[0]
    owner_rows = local_rows * col_count
    owner_blocks = owner_rows // block_size
    stripe_rows = local_rows * row_count
    stripe_blocks = stripe_rows // block_size
    answers = local_rows * row_count * col_count
    stripe_probe = lax.all_gather(probe, "row", axis=0, tiled=True)
    partial_value = slot_product(
        blocks, (stripe_probe,), jnp.zeros((1,), jnp.int32), block_row, block_col, counts,
        owner_rows, False,
    )
    local_start = lax.axis_index("col") * local_rows
    local_weight = lax.dynamic_slice_in_dim(self_weight, local_start, local_rows, 0)
    own_rows = lax.dynamic_slice_in_dim(partial_value, local_start, local_rows, 0)
    partial_value = lax.dynamic_update_slice_in_dim(
        partial_value, own_rows + local_weight[:, None] * probe, local_start, 0
    )
    part, other, inner = pair_all_reduce(partial_value, "col", col_count)
    inner = jnp.reshape(inner, (1,)).astype(jnp.int32)
    if other is None:
        sources = (part,)
        projected = lax.dynamic_slice_in_dim(part, local_start, local_rows, 0)
    else:
        sources = (part, other)
        half_rows = part.shape[0]
        offset = local_start % half_rows
        projected = jnp.where(
            local_start // half_rows == inner[0],
            lax.dynamic_slice_in_dim(part, offset, local_rows, 0),
            lax.dynamic_slice_in_dim(other, offset, local_rows, 0),
        )
    w_partial = slot_product(
        blocks, sources, inner, block_row, block_col, counts, stripe_rows, True
    )
    w_share = lax.psum_scatter(w_partial, "row", scatter_dimension=0, tiled=True)
    sketch = local_weight[:, None] * projected + w_share
    gram_part = jnp.dot(sketch.T, sketch, precision=PRECISE, preferred_element_type=jnp.float32)
    gram = butterfly_sum(gram_part, ("row", "col"), row_count * col_count)
    lower = jnp.linalg.cholesky(gram)
    solved = lax.linalg.triangular_solve(
        lower, sketch, left_side=False, lower=True, transpose_a=True
    )
    basis = solved * math.sqrt(answers)
    return (projected, basis)


def solution(mesh):
    in_specs = (
        P(("row", "col"), None),
        P("row"),
        P(("row", "col"), None, None),
        P(("row", "col")),
        P(("row", "col")),
        P(("row", "col")),
    )
    out_specs = (P(("row", "col"), None), P(("row", "col"), None))
    return jax.shard_map(shards, mesh=mesh, in_specs=in_specs, out_specs=out_specs, check_vma=False)
```
